32 devices in a mesh: cases: 2 (over y), blk: 8 (over z, x), state: 2 (over core).
Axes of the slice: x: 2, y: 2, z: 4, core: 2. Of those that a mesh axis runs over, the one named last changes fastest.
Arguments:
- base_real: float32 [32768], P(('cases', 'blk', 'state')), parts along dimension 0, may hold values from -6 to 6
- base_reactive: float32 [32768], P(('cases', 'blk', 'state')), parts along dimension 0, may hold values from 0.2 to 1
- voltage: float32 [32768], P(('cases', 'blk', 'state')), parts along dimension 0, may hold values from 0.9 to 1.1
- rating: float32 [32768], P(('cases', 'blk', 'state')), parts along dimension 0, may hold values from 1 to 4
- monitored: int32 [16384], P(('cases', 'blk', 'state')), parts along dimension 0, may hold values from 0 to 2047, as said below
- tile_ids: int32 [128, 4], P(('cases', 'blk', 'state')), parts along dimension 0, may hold values from -1 to 7, as said below
- tile_values: bfloat16 [128, 4, 128, 128], P(('cases', 'blk', 'state')), parts along dimension 0, may hold values from -0.5 to 0.5
- outage_ids: int32 [16, 128], P(('cases', 'blk')), parts along dimension 0, may hold values from 0 to 2047, as said below
- coupling: bfloat16 [16, 128, 128], P(('cases', 'blk')), parts along dimension 0, may hold values from -0.5 to 0.5
- outage_pairs: int32 [16, 2, 128], P(('cases', 'blk')), parts along dimension 0, may hold values from 0 to 127, as said below
Outputs:
- branch_peak: float32 [16384], P(('cases', 'blk', 'state')), parts along dimension 0
- worst_loading: float32 [16, 128], P(('cases', 'blk'), 'state'), parts along dimension 0
The draws below stay inside these ranges and needn't reach their ends.
There are 2 independent parts, one for each index of `cases`. The reference program is written for one: setup_inputs(seed, part) draws one part's arguments, and reference() takes and returns one part's arrays. A program takes and returns all parts, laid end to end along the dimension named above; each array names one. Nothing has to cross between parts.
Inputs may be any that keep to these rules, and one draw needn't show every extreme that they name: `monitored`: the 1024 entries of one cycle position (entry index // 1024) are distinct. `outage_ids`: each row holds 128 distinct indices. `tile_ids`: each row names between 2 and 4 distinct outage blocks in its first slots and holds -1 in the remaining slots; some row is full. `outage_pairs`: the two branches of a pair differ.
All inputs are finite; a program needn't handle non-finite values.
Results may differ from the reference program's by a relative error of at most 0.0019.
Values may be sent and summed in bfloat16 or wider, within the bound.
No kernel may reach another device: no remote copies, remote signals or barrier semaphores. Data moves between devices by JAX's collectives and lax.ppermute only.
A program may use at most 64 MiB of HBM per device.

```python
import math
import jax
import jax.numpy as jnp
from jax import lax

TILE = 128
PAIRS = 128
NBLK = 8
KB = 4
BR_POS = 2048
MON_POS = 1024
BRANCHES = 16384
MON = 8192
MON_TILES = 64


def swap_in(order, value, slot):
    where_at = jnp.argmax(order == value)
    displaced = order[slot]
    order = order.at[where_at].set(displaced)
    return order.at[slot].set(value)


def chosen_rows(key, row_count, span, keep):
    keys = jax.random.split(key, row_count)
    orders = jax.vmap(lambda one_key: jax.random.permutation(one_key, span))(keys).astype(jnp.int32)
    picked = jax.random.randint(jax.random.fold_in(key, 5), (), 0, row_count)
    forced = swap_in(swap_in(orders[picked], 0, 0), span - 1, 1)
    orders = orders.at[picked].set(forced)
    return orders[:, :keep]


def draw_monitored(key, part):
    rows_out = chosen_rows(jax.random.fold_in(key, 11), NBLK, BR_POS, MON_POS)
    return rows_out.reshape(MON).astype(jnp.int32)


def draw_outage_ids(key, part):
    return chosen_rows(jax.random.fold_in(key, 23), NBLK, BR_POS, TILE).astype(jnp.int32)


def draw_tile_ids(key, part):
    base_key = jax.random.fold_in(key, 31)
    orders = chosen_rows(base_key, MON_TILES, NBLK, KB)
    counts = jax.random.randint(jax.random.fold_in(base_key, 7), (MON_TILES,), KB // 2, KB + 1)
    full_row = jax.random.randint(jax.random.fold_in(base_key, 9), (), 0, MON_TILES)
    counts = counts.at[full_row].set(KB)
    counts = counts.at[(full_row + 1) % MON_TILES].set(KB // 2)
    slots = jnp.arange(KB, dtype=jnp.int32)[None, :]
    return jnp.where(slots < counts[:, None], orders, -1).astype(jnp.int32)


def draw_outage_pairs(key, part):
    base_key = jax.random.fold_in(key, 37)
    first_idx = jax.random.randint(jax.random.fold_in(base_key, 1), (NBLK, PAIRS), 0, TILE)
    offset = jax.random.randint(jax.random.fold_in(base_key, 2), (NBLK, PAIRS), 1, TILE)
    second_idx = (first_idx + offset) % TILE
    return jnp.stack([first_idx, second_idx], axis=1).astype(jnp.int32)


def block_scale(own_key, shape, shards, least, high):
    loudness = 1.0
    for axis_at, shards_of in shards:
        steps = jax.random.uniform(jax.random.fold_in(jax.random.fold_in(own_key, 6), axis_at), (shards_of,), jnp.float32, least / len(shards), high / len(shards))
        loudness = loudness * jnp.repeat(jnp.exp(steps), shape[axis_at] // shards_of).reshape((-1,) + (1,) * (len(shape) - 1 - axis_at))
    return loudness


def normal_values(own_key, dims, scale, limit, shards=(), kind=jnp.bfloat16):
    values = scale * jax.random.normal(own_key, dims, jnp.float32)
    if shards:
        values = values * block_scale(own_key, dims, shards, -0.22, 0.18)
    return jnp.clip(values, -limit, limit).astype(kind)


def setup_inputs(seed: int = 0, part: int = 0) -> dict:
    arg_keys = jax.random.split(jax.random.key(seed), 11)
    part_splits = jax.random.split(jax.random.fold_in(arg_keys[10], part), 11)
    return {
        "base_real": normal_values(part_splits[0], (BRANCHES,), 1.0, 6.0, ((0, 16),), jnp.float32),
        "base_reactive": jnp.clip(0.2 + 0.8 * jax.random.uniform(part_splits[1], (BRANCHES,), jnp.float32) ** block_scale(part_splits[1], (BRANCHES,), ((0, 16),), -0.2, 0.2), 0.2, 1.0),
        "voltage": jnp.clip(0.9 + 0.20000005 * jax.random.uniform(part_splits[2], (BRANCHES,), jnp.float32) ** block_scale(part_splits[2], (BRANCHES,), ((0, 16),), -0.2, 0.2), 0.9, 1.1),
        "rating": jnp.clip(jnp.exp(math.log(4.0) - 1.3862944 * jax.random.uniform(part_splits[3], (BRANCHES,), jnp.float32) ** block_scale(part_splits[3], (BRANCHES,), ((0, 16),), -0.2, 0.2)), 1.0, 4.0),
        "monitored": draw_monitored(jax.random.fold_in(jax.random.fold_in(arg_keys[10], part), 71), part),
        "tile_ids": draw_tile_ids(jax.random.fold_in(jax.random.fold_in(arg_keys[10], part), 71), part),
        "tile_values": jnp.clip(jax.random.uniform(part_splits[6], (MON_TILES, KB, TILE, TILE), jnp.float32, -0.5, 0.5) * block_scale(part_splits[6], (MON_TILES, KB, TILE, TILE), ((0, 16),), -0.4, 0.0), -0.5, 0.5).astype(jnp.bfloat16),
        "outage_ids": draw_outage_ids(jax.random.fold_in(jax.random.fold_in(arg_keys[10], part), 71), part),
        "coupling": jnp.clip(jax.random.uniform(part_splits[8], (NBLK, TILE, TILE), jnp.float32, -0.5, 0.5) * block_scale(part_splits[8], (NBLK, TILE, TILE), ((0, 8),), -0.4, 0.0), -0.5, 0.5).astype(jnp.bfloat16),
        "outage_pairs": draw_outage_pairs(jax.random.fold_in(jax.random.fold_in(arg_keys[10], part), 71), part),
    }


def reference(base_real, base_reactive, voltage, rating, monitored, tile_ids, tile_values, outage_ids, coupling, outage_pairs):
    position = jnp.arange(MON, dtype=jnp.int32) // MON_POS
    branch_number = (position * BR_POS + monitored).astype(jnp.int32)
    mon_real = base_real[branch_number].reshape(MON_TILES, TILE)
    mon_reactive = base_reactive[branch_number].reshape(MON_TILES, TILE)
    mon_limit = (voltage[branch_number] * rating[branch_number]).reshape(MON_TILES, TILE)
    react_sq = mon_reactive * mon_reactive
    block_base = jnp.arange(NBLK, dtype=jnp.int32)[:, None] * BR_POS
    outage_flow = base_real[(block_base + outage_ids).astype(jnp.int32)].astype(jnp.bfloat16)
    first_idx = outage_pairs[:, 0, :]
    second_idx = outage_pairs[:, 1, :]
    flow_first = jnp.take_along_axis(outage_flow, first_idx, axis=1).astype(jnp.float32)
    flow_second = jnp.take_along_axis(outage_flow, second_idx, axis=1).astype(jnp.float32)
    block_rows = jnp.arange(NBLK, dtype=jnp.int32)[:, None]
    s_first_second = coupling[block_rows, first_idx, second_idx].astype(jnp.float32)
    s_second_first = coupling[block_rows, second_idx, first_idx].astype(jnp.float32)
    determinant = 1.0 - s_first_second * s_second_first
    w_first = (flow_first + s_first_second * flow_second) / determinant
    w_second = (flow_second + s_second_first * flow_first) / determinant
    matches = tile_ids[:, :, None] == jnp.arange(NBLK, dtype=jnp.int32)[None, None, :]
    slot_table = lax.optimization_barrier(jnp.sum(jnp.where(matches, jnp.arange(KB, dtype=jnp.int32)[None, :, None], 0), axis=1)).astype(jnp.int32)
    present = jnp.any(matches, axis=1)
    rows_iota = lax.broadcasted_iota(jnp.int32, (TILE, PAIRS), 0)
    tile_rows = jnp.arange(MON_TILES, dtype=jnp.int32)

    def per_block(block_now):
        pair_first = first_idx[block_now]
        pair_second = second_idx[block_now]
        weights = (jnp.where(rows_iota == pair_first[None, :], w_first[block_now][None, :], 0.0) + jnp.where(rows_iota == pair_second[None, :], w_second[block_now][None, :], 0.0)).astype(jnp.bfloat16)
        chosen = tile_values[tile_rows, slot_table[:, block_now]].astype(jnp.float32)
        delta = jnp.einsum('tmi,ip->tmp', chosen, weights.astype(jnp.float32), precision=lax.Precision.HIGHEST)
        delta = jnp.where(present[:, block_now][:, None, None], delta, 0.0)
        post = mon_real[:, :, None] + delta
        loading = jnp.sqrt(post * post + react_sq[:, :, None]) / mon_limit[:, :, None]
        return (lax.optimization_barrier(jnp.max(loading, axis=2)), lax.optimization_barrier(jnp.max(loading, axis=(0, 1))))
    peaks, worsts = lax.map(per_block, jnp.arange(NBLK, dtype=jnp.int32))
    branch_peak = lax.optimization_barrier(jnp.max(peaks, axis=0)).reshape(MON)
    return (branch_peak, worsts)
```

```python
import jax
import jax.numpy as jnp
from jax import lax
from jax.sharding import PartitionSpec as P


def gather_shifts(x, axis):
    n = lax.axis_size(axis)
    parts = [x]
    for k in range(1, n):
        perm = [(j, (j + k) % n) for j in range(n)]
        parts.append(lax.ppermute(x, axis, perm))
    return jnp.stack(parts)


def gather_ordered(x, axis):
    n = lax.axis_size(axis)
    me = lax.axis_index(axis)
    stacked = gather_shifts(x, axis)
    return jnp.take(stacked, (me - jnp.arange(n)) % n, axis=0)


def scatter_max(x, axis):
    n = lax.axis_size(axis)
    me = lax.axis_index(axis)
    result = lax.dynamic_index_in_dim(x, me, 0, keepdims=False)
    for k in range(1, n):
        perm = [(j, (j + k) % n) for j in range(n)]
        piece = lax.dynamic_index_in_dim(x, (me + k) % n, 0, keepdims=False)
        result = jnp.maximum(result, lax.ppermute(piece, axis, perm))
    return result


def solve_pairs(flows_block, coupling_block, pair_block):
    first_idx = pair_block[0]
    second_idx = pair_block[1]
    flow_first = jnp.take(flows_block, first_idx).astype(jnp.float32)
    flow_second = jnp.take(flows_block, second_idx).astype(jnp.float32)
    s_first_second = coupling_block[first_idx, second_idx].astype(jnp.float32)
    s_second_first = coupling_block[second_idx, first_idx].astype(jnp.float32)
    determinant = 1.0 - s_first_second * s_second_first
    w_first = (flow_first + s_first_second * flow_second) / determinant
    w_second = (flow_second + s_second_first * flow_first) / determinant
    return (w_first, w_second)


def body(
    base_real,
    base_reactive,
    voltage,
    rating,
    monitored,
    tile_ids,
    tile_values,
    outage_ids,
    coupling,
    outage_pairs,
):
    tiles_dev, slot_count, tile_size, _ = tile_values.shape
    pair_count = outage_pairs.shape[2]
    blocks = lax.axis_size("blk")
    halves = lax.axis_size("state")
    half_width = pair_count // halves
    me_blk = lax.axis_index("blk")

    state_local = jnp.stack([base_real, base_reactive, voltage, rating])
    state_pos = gather_ordered(state_local, "state")
    state_pos = jnp.moveaxis(state_pos, 0, 1).reshape(4, -1)
    real_pos = state_pos[0]

    outage_flow = jnp.take(real_pos, outage_ids[0]).astype(jnp.bfloat16)
    own_first, own_second = solve_pairs(outage_flow, coupling[0], outage_pairs[0])
    packed = jnp.stack(
        [
            own_first,
            own_second,
            outage_pairs[0, 0].astype(jnp.float32),
            outage_pairs[0, 1].astype(jnp.float32),
        ]
    )
    shifted = gather_shifts(packed, "blk")

    mon_vals = jnp.take(state_pos, monitored, axis=1).reshape(4, tiles_dev, tile_size)
    mon_real = mon_vals[0]
    react_sq = mon_vals[1] * mon_vals[1]
    mon_limit = mon_vals[2] * mon_vals[3]

    valid = tile_ids >= 0
    block_of = jnp.clip(tile_ids, 0, blocks - 1)
    chosen = jnp.take(shifted, (me_blk - block_of) % blocks, axis=0)
    rows_iota = lax.broadcasted_iota(jnp.int32, (1, 1, tile_size, pair_count), 2)
    first_at = chosen[:, :, 2].astype(jnp.int32)[:, :, None, :]
    second_at = chosen[:, :, 3].astype(jnp.int32)[:, :, None, :]
    w_first = chosen[:, :, 0].astype(jnp.bfloat16)[:, :, None, :]
    w_second = chosen[:, :, 1].astype(jnp.bfloat16)[:, :, None, :]
    zero = jnp.zeros((), jnp.bfloat16)
    weights = jnp.where(rows_iota == first_at, w_first, zero) + jnp.where(
        rows_iota == second_at, w_second, zero
    )
    delta = jnp.einsum(
        "tkmi,tkip->tkmp", tile_values, weights, preferred_element_type=jnp.float32
    )
    post = mon_real[:, None, :, None] + delta
    loading = jnp.sqrt(post * post + react_sq[:, None, :, None]) / mon_limit[:, None, :, None]
    neg = jnp.float32(-jnp.inf)
    loading = jnp.where(valid[:, :, None, None], loading, neg)

    base_load = jnp.sqrt(mon_real * mon_real + react_sq) / mon_limit
    block_iota = jnp.arange(blocks, dtype=jnp.int32)
    matches = tile_ids[:, :, None] == block_iota[None, None, :]
    absent = jnp.logical_not(jnp.any(matches, axis=1))
    any_absent = jnp.any(absent, axis=1)

    peak_load = jnp.max(loading, axis=(1, 3))
    peak_load = jnp.maximum(peak_load, jnp.where(any_absent[:, None], base_load, neg))

    col_max = jnp.max(loading, axis=2)
    worst_local = jnp.max(
        jnp.where(matches[:, :, :, None], col_max[:, :, None, :], neg), axis=(0, 1)
    )
    base_max = jnp.max(base_load, axis=1)
    absent_max = jnp.max(jnp.where(absent, base_max[:, None], neg), axis=0)
    worst_local = jnp.maximum(worst_local, absent_max[:, None])

    by_half = worst_local.reshape(blocks, halves, half_width).transpose(1, 0, 2)
    half_max = scatter_max(by_half, "state")
    worst_own = scatter_max(half_max, "blk")[None, :]
    return (peak_load.reshape(-1), worst_own)


def solution(mesh):
    return jax.shard_map(
        body,
        mesh=mesh,
        in_specs=(
            P(("cases", "blk", "state")),
            P(("cases", "blk", "state")),
            P(("cases", "blk", "state")),
            P(("cases", "blk", "state")),
            P(("cases", "blk", "state")),
            P(("cases", "blk", "state"), None),
            P(("cases", "blk", "state"), None, None, None),
            P(("cases", "blk"), None),
            P(("cases", "blk"), None, None),
            P(("cases", "blk"), None, None),
        ),
        out_specs=(P(("cases", "blk", "state")), P(("cases", "blk"), "state")),
        check_vma=False,
    )
```

```python
import jax
import jax.numpy as jnp
from jax import lax
from jax.sharding import PartitionSpec as P


def axes_size(axes):
    size = 1
    for axis in axes:
        size *= lax.axis_size(axis)
    return size


def gather_doubling(x, axes):
    n = axes_size(axes)
    me = lax.axis_index(axes)
    cur = x[None]
    bit = 1
    while bit < n:
        other = lax.ppermute(cur, axes, [(j, j ^ bit) for j in range(n)])
        low = (me & bit) == 0
        cur = jnp.where(low, jnp.concatenate([cur, other]), jnp.concatenate([other, cur]))
        bit *= 2
    return cur


def scatter_max(x, axes):
    n = axes_size(axes)
    me = lax.axis_index(axes)
    cur = x
    bit = 1
    while bit < n:
        pairs = cur.reshape((cur.shape[0] // 2, 2) + cur.shape[1:])
        mine = (me // bit) % 2
        keep = lax.dynamic_index_in_dim(pairs, mine, 1, keepdims=False)
        send = lax.dynamic_index_in_dim(pairs, 1 - mine, 1, keepdims=False)
        cur = jnp.maximum(keep, lax.ppermute(send, axes, [(j, j ^ bit) for j in range(n)]))
        bit *= 2
    return cur[0]


def body(
    base_real,
    base_reactive,
    voltage,
    rating,
    monitored,
    tile_ids,
    tile_values,
    outage_ids,
    coupling,
    outage_pairs,
):
    tiles_dev, slot_count, tile_size, _ = tile_values.shape
    pair_count = outage_pairs.shape[2]
    blocks = lax.axis_size("blk")
    halves = lax.axis_size("state")
    half_width = pair_count // halves
    half_len = base_real.shape[0]
    me_state = lax.axis_index("state")
    both = ("blk", "state")

    first_idx = outage_pairs[0, 0]
    second_idx = outage_pairs[0, 1]
    local_at = outage_ids[0] - me_state * half_len
    in_half = (local_at >= 0) & (local_at < half_len)
    flow_part = jnp.where(in_half, jnp.take(base_real, jnp.clip(local_at, 0, half_len - 1)), 0.0)
    flow_part = flow_part.astype(jnp.bfloat16).astype(jnp.float32)
    pair_at = jnp.concatenate([first_idx, second_idx])
    flow_pairs = jnp.take(flow_part, pair_at).reshape(2, pair_count)
    coupled = coupling[0][pair_at, jnp.concatenate([second_idx, first_idx])]
    coupled = coupled.astype(jnp.float32).reshape(2, pair_count)
    packed = jnp.concatenate(
        [flow_pairs, coupled, outage_pairs[0].astype(jnp.float32)]
    )
    known = gather_doubling(packed, both).reshape(blocks, halves, 6, pair_count)

    state_local = jnp.stack([base_real, base_reactive, voltage, rating])
    other_half = lax.ppermute(
        state_local, "state", [(j, (j + 1) % halves) for j in range(halves)]
    )
    state_pos = jnp.where(
        me_state == 0,
        jnp.concatenate([state_local, other_half], axis=1),
        jnp.concatenate([other_half, state_local], axis=1),
    )
    mon_vals = jnp.take(state_pos, monitored, axis=1).reshape(4, tiles_dev, tile_size)
    mon_real = mon_vals[0]
    react_sq = mon_vals[1] * mon_vals[1]
    mon_limit = mon_vals[2] * mon_vals[3]

    flow_first = jnp.sum(known[:, :, 0], axis=1)
    flow_second = jnp.sum(known[:, :, 1], axis=1)
    s_first_second = known[:, 0, 2]
    s_second_first = known[:, 0, 3]
    determinant = 1.0 - s_first_second * s_second_first
    w_first_all = (flow_first + s_first_second * flow_second) / determinant
    w_second_all = (flow_second + s_second_first * flow_first) / determinant
    table = jnp.stack([w_first_all, w_second_all, known[:, 0, 4], known[:, 0, 5]], axis=1)

    valid = tile_ids >= 0
    block_of = jnp.clip(tile_ids, 0, blocks - 1)
    chosen = jnp.take(table, block_of, axis=0)
    rows_iota = lax.broadcasted_iota(jnp.int32, (1, 1, tile_size, pair_count), 2)
    first_at = chosen[:, :, 2].astype(jnp.int32)[:, :, None, :]
    second_at = chosen[:, :, 3].astype(jnp.int32)[:, :, None, :]
    w_first = chosen[:, :, 0].astype(jnp.bfloat16)[:, :, None, :]
    w_second = chosen[:, :, 1].astype(jnp.bfloat16)[:, :, None, :]
    zero = jnp.zeros((), jnp.bfloat16)
    weights = jnp.where(rows_iota == first_at, w_first, zero) + jnp.where(
        rows_iota == second_at, w_second, zero
    )
    delta = jnp.einsum(
        "tkmi,tkip->tkmp", tile_values, weights, preferred_element_type=jnp.float32
    )
    post = mon_real[:, None, :, None] + delta
    loading = jnp.sqrt(post * post + react_sq[:, None, :, None]) / mon_limit[:, None, :, None]
    neg = jnp.float32(-jnp.inf)
    loading = jnp.where(valid[:, :, None, None], loading, neg)

    base_load = jnp.sqrt(mon_real * mon_real + react_sq) / mon_limit
    block_iota = jnp.arange(blocks, dtype=jnp.int32)
    matches = tile_ids[:, :, None] == block_iota[None, None, :]
    absent = jnp.logical_not(jnp.any(matches, axis=1))
    any_absent = jnp.any(absent, axis=1)

    peak_load = jnp.max(loading, axis=(1, 3))
    peak_load = jnp.maximum(peak_load, jnp.where(any_absent[:, None], base_load, neg))

    col_max = jnp.max(loading, axis=2)
    worst_local = jnp.max(
        jnp.where(matches[:, :, :, None], col_max[:, :, None, :], neg), axis=(0, 1)
    )
    base_max = jnp.max(base_load, axis=1)
    absent_max = jnp.max(jnp.where(absent, base_max[:, None], neg), axis=0)
    worst_local = jnp.maximum(worst_local, absent_max[:, None])

    worst_own = scatter_max(worst_local.reshape(blocks * halves, half_width), both)[None, :]
    return (peak_load.reshape(-1), worst_own)


def solution(mesh):
    return jax.shard_map(
        body,
        mesh=mesh,
        in_specs=(
            P(("cases", "blk", "state")),
            P(("cases", "blk", "state")),
            P(("cases", "blk", "state")),
            P(("cases", "blk", "state")),
            P(("cases", "blk", "state")),
            P(("cases", "blk", "state"), None),
            P(("cases", "blk", "state"), None, None, None),
            P(("cases", "blk"), None),
            P(("cases", "blk"), None, None),
            P(("cases", "blk"), None, None),
        ),
        out_specs=(P(("cases", "blk", "state")), P(("cases", "blk"), "state")),
        check_vma=False,
    )
```

```python
import jax
import jax.numpy as jnp
from jax import lax
from jax.sharding import PartitionSpec as P


def axes_size(axes):
    size = 1
    for axis in axes:
        size *= lax.axis_size(axis)
    return size


def gather_doubling(x, axes):
    n = axes_size(axes)
    me = lax.axis_index(axes)
    cur = x[None]
    bit = 1
    while bit < n:
        other = lax.ppermute(cur, axes, [(j, j ^ bit) for j in range(n)])
        low = (me & bit) == 0
        cur = jnp.where(low, jnp.concatenate([cur, other]), jnp.concatenate([other, cur]))
        bit *= 2
    return cur


def scatter_max(x, axes):
    n = axes_size(axes)
    me = lax.axis_index(axes)
    cur = x
    bit = 1
    while bit < n:
        pairs = cur.reshape((cur.shape[0] // 2, 2) + cur.shape[1:])
        mine = (me // bit) % 2
        keep = lax.dynamic_index_in_dim(pairs, mine, 1, keepdims=False)
        send = lax.dynamic_index_in_dim(pairs, 1 - mine, 1, keepdims=False)
        cur = jnp.maximum(keep, lax.ppermute(send, axes, [(j, j ^ bit) for j in range(n)]))
        bit *= 2
    return cur[0]


def body(
    base_real,
    base_reactive,
    voltage,
    rating,
    monitored,
    tile_ids,
    tile_values,
    outage_ids,
    coupling,
    outage_pairs,
):
    tiles_dev, slot_count, tile_size, _ = tile_values.shape
    pair_count = outage_pairs.shape[2]
    blocks = lax.axis_size("blk")
    halves = lax.axis_size("state")
    half_width = pair_count // halves
    half_len = base_real.shape[0]
    me_state = lax.axis_index("state")
    both = ("blk", "state")

    first_idx = outage_pairs[0, 0]
    second_idx = outage_pairs[0, 1]
    local_at = outage_ids[0] - me_state * half_len
    branch_iota = lax.broadcasted_iota(jnp.int32, (pair_count, half_len), 1)
    pick_branch = (branch_iota == local_at[:, None]).astype(jnp.bfloat16)
    flow_part = jnp.dot(
        pick_branch, base_real.astype(jnp.bfloat16), preferred_element_type=jnp.float32
    )
    pair_at = jnp.concatenate([first_idx, second_idx])
    pair_to = jnp.concatenate([second_idx, first_idx])
    outage_iota = lax.broadcasted_iota(jnp.int32, (2 * pair_count, pair_count), 1)
    pick_at = (outage_iota == pair_at[:, None]).astype(jnp.bfloat16)
    flow_pairs = jnp.dot(
        pick_at, flow_part.astype(jnp.bfloat16), preferred_element_type=jnp.float32
    ).reshape(2, pair_count)
    coupled_rows = jnp.dot(pick_at, coupling[0], preferred_element_type=jnp.float32)
    coupled = jnp.sum(
        jnp.where(outage_iota == pair_to[:, None], coupled_rows, 0.0), axis=1
    ).reshape(2, pair_count)
    packed = jnp.concatenate(
        [flow_pairs, coupled, outage_pairs[0].astype(jnp.float32)]
    )
    known = gather_doubling(packed, both).reshape(blocks, halves, 6, pair_count)

    state_local = jnp.stack([base_real, base_reactive, voltage, rating])
    other_half = lax.ppermute(
        state_local, "state", [(j, (j + 1) % halves) for j in range(halves)]
    )
    state_pos = jnp.where(
        me_state == 0,
        jnp.concatenate([state_local, other_half], axis=1),
        jnp.concatenate([other_half, state_local], axis=1),
    )
    mon_vals = jnp.take(state_pos, monitored, axis=1).reshape(4, tiles_dev, tile_size)
    mon_real = mon_vals[0]
    react_sq = mon_vals[1] * mon_vals[1]
    mon_limit = mon_vals[2] * mon_vals[3]

    flow_first = jnp.sum(known[:, :, 0], axis=1)
    flow_second = jnp.sum(known[:, :, 1], axis=1)
    s_first_second = known[:, 0, 2]
    s_second_first = known[:, 0, 3]
    determinant = 1.0 - s_first_second * s_second_first
    w_first_all = (flow_first + s_first_second * flow_second) / determinant
    w_second_all = (flow_second + s_second_first * flow_first) / determinant
    table = jnp.stack([w_first_all, w_second_all, known[:, 0, 4], known[:, 0, 5]], axis=1)

    valid = tile_ids >= 0
    block_of = jnp.clip(tile_ids, 0, blocks - 1)
    chosen = jnp.take(table, block_of, axis=0)
    rows_iota = lax.broadcasted_iota(jnp.int32, (1, 1, tile_size, pair_count), 2)
    first_at = chosen[:, :, 2].astype(jnp.int32)[:, :, None, :]
    second_at = chosen[:, :, 3].astype(jnp.int32)[:, :, None, :]
    w_first = chosen[:, :, 0].astype(jnp.bfloat16)[:, :, None, :]
    w_second = chosen[:, :, 1].astype(jnp.bfloat16)[:, :, None, :]
    zero = jnp.zeros((), jnp.bfloat16)
    weights = jnp.where(rows_iota == first_at, w_first, zero) + jnp.where(
        rows_iota == second_at, w_second, zero
    )
    delta = jnp.einsum(
        "tkmi,tkip->tkmp", tile_values, weights, preferred_element_type=jnp.float32
    )
    post = mon_real[:, None, :, None] + delta
    loading = jnp.sqrt(post * post + react_sq[:, None, :, None]) / mon_limit[:, None, :, None]
    neg = jnp.float32(-jnp.inf)
    loading = jnp.where(valid[:, :, None, None], loading, neg)

    base_load = jnp.sqrt(mon_real * mon_real + react_sq) / mon_limit
    block_iota = jnp.arange(blocks, dtype=jnp.int32)
    matches = tile_ids[:, :, None] == block_iota[None, None, :]
    absent = jnp.logical_not(jnp.any(matches, axis=1))
    any_absent = jnp.any(absent, axis=1)

    peak_load = jnp.max(loading, axis=(1, 3))
    peak_load = jnp.maximum(peak_load, jnp.where(any_absent[:, None], base_load, neg))

    col_max = jnp.max(loading, axis=2)
    worst_local = jnp.max(
        jnp.where(matches[:, :, :, None], col_max[:, :, None, :], neg), axis=(0, 1)
    )
    base_max = jnp.max(base_load, axis=1)
    absent_max = jnp.max(jnp.where(absent, base_max[:, None], neg), axis=0)
    worst_local = jnp.maximum(worst_local, absent_max[:, None])

    worst_own = scatter_max(worst_local.reshape(blocks * halves, half_width), both)[None, :]
    return (peak_load.reshape(-1), worst_own)


def solution(mesh):
    return jax.shard_map(
        body,
        mesh=mesh,
        in_specs=(
            P(("cases", "blk", "state")),
            P(("cases", "blk", "state")),
            P(("cases", "blk", "state")),
            P(("cases", "blk", "state")),
            P(("cases", "blk", "state")),
            P(("cases", "blk", "state"), None),
            P(("cases", "blk", "state"), None, None, None),
            P(("cases", "blk"), None),
            P(("cases", "blk"), None, None),
            P(("cases", "blk"), None, None),
        ),
        out_specs=(P(("cases", "blk", "state")), P(("cases", "blk"), "state")),
        check_vma=False,
    )
```

```python
import jax
import jax.numpy as jnp
from jax import lax
from jax.sharding import PartitionSpec as P


def axes_size(axes):
    size = 1
    for axis in axes:
        size *= lax.axis_size(axis)
    return size


def gather_doubling(x, axes):
    n = axes_size(axes)
    me = lax.axis_index(axes)
    cur = x[None]
    bit = 1
    while bit < n:
        other = lax.ppermute(cur, axes, [(j, j ^ bit) for j in range(n)])
        low = (me & bit) == 0
        cur = jnp.where(low, jnp.concatenate([cur, other]), jnp.concatenate([other, cur]))
        bit *= 2
    return cur


def scatter_max(x, axes):
    n = axes_size(axes)
    me = lax.axis_index(axes)
    cur = x
    bit = 1
    while bit < n:
        pairs = cur.reshape((cur.shape[0] // 2, 2) + cur.shape[1:])
        mine = (me // bit) % 2
        keep = lax.dynamic_index_in_dim(pairs, mine, 1, keepdims=False)
        send = lax.dynamic_index_in_dim(pairs, 1 - mine, 1, keepdims=False)
        cur = jnp.maximum(keep, lax.ppermute(send, axes, [(j, j ^ bit) for j in range(n)]))
        bit *= 2
    return cur[0]


def body(
    base_real,
    base_reactive,
    voltage,
    rating,
    monitored,
    tile_ids,
    tile_values,
    outage_ids,
    coupling,
    outage_pairs,
):
    tiles_dev, slot_count, tile_size, _ = tile_values.shape
    pair_count = outage_pairs.shape[2]
    blocks = lax.axis_size("blk")
    halves = lax.axis_size("state")
    half_width = pair_count // halves
    half_len = base_real.shape[0]
    me_state = lax.axis_index("state")
    both = ("blk", "state")

    first_idx = outage_pairs[0, 0]
    second_idx = outage_pairs[0, 1]
    local_at = outage_ids[0] - me_state * half_len
    branch_iota = lax.broadcasted_iota(jnp.int32, (pair_count, half_len), 1)
    pick_branch = (branch_iota == local_at[:, None]).astype(jnp.bfloat16)
    flow_part = jnp.dot(
        pick_branch, base_real.astype(jnp.bfloat16), preferred_element_type=jnp.float32
    )
    pair_at = jnp.concatenate([first_idx, second_idx])
    pair_to = jnp.concatenate([second_idx, first_idx])
    outage_iota = lax.broadcasted_iota(jnp.int32, (2 * pair_count, pair_count), 1)
    pick_at = (outage_iota == pair_at[:, None]).astype(jnp.bfloat16)
    flow_pairs = jnp.dot(
        pick_at, flow_part.astype(jnp.bfloat16), preferred_element_type=jnp.float32
    ).reshape(2, pair_count)
    coupled_rows = jnp.dot(pick_at, coupling[0], preferred_element_type=jnp.float32)
    coupled = jnp.sum(
        jnp.where(outage_iota == pair_to[:, None], coupled_rows, 0.0), axis=1
    ).reshape(2, pair_count)
    packed = jnp.concatenate(
        [flow_pairs, coupled, outage_pairs[0].astype(jnp.float32)]
    )
    known = gather_doubling(packed, both).reshape(blocks, halves, 6, pair_count)

    state_local = jnp.stack(
        [base_real, base_reactive * base_reactive, voltage * rating], axis=1
    )
    other_half = lax.ppermute(
        state_local, "state", [(j, (j + 1) % halves) for j in range(halves)]
    )
    state_pos = jnp.concatenate([state_local, other_half])
    mon_at = (monitored - me_state * half_len) % (halves * half_len)
    mon_vals = jnp.take(state_pos, mon_at, axis=0, mode="clip")
    mon_real = mon_vals[:, 0].reshape(tiles_dev, tile_size)
    react_sq = mon_vals[:, 1].reshape(tiles_dev, tile_size)
    mon_limit = mon_vals[:, 2].reshape(tiles_dev, tile_size)

    flow_first = jnp.sum(known[:, :, 0], axis=1)
    flow_second = jnp.sum(known[:, :, 1], axis=1)
    s_first_second = known[:, 0, 2]
    s_second_first = known[:, 0, 3]
    determinant = 1.0 - s_first_second * s_second_first
    w_first_all = (flow_first + s_first_second * flow_second) / determinant
    w_second_all = (flow_second + s_second_first * flow_first) / determinant
    table = jnp.stack([w_first_all, w_second_all, known[:, 0, 4], known[:, 0, 5]], axis=1)

    valid = tile_ids >= 0
    block_of = jnp.clip(tile_ids, 0, blocks - 1)
    chosen = jnp.take(table, block_of, axis=0)
    rows_iota = lax.broadcasted_iota(jnp.int32, (1, 1, tile_size, pair_count), 2)
    first_at = chosen[:, :, 2].astype(jnp.int32)[:, :, None, :]
    second_at = chosen[:, :, 3].astype(jnp.int32)[:, :, None, :]
    w_first = chosen[:, :, 0].astype(jnp.bfloat16)[:, :, None, :]
    w_second = chosen[:, :, 1].astype(jnp.bfloat16)[:, :, None, :]
    zero = jnp.zeros((), jnp.bfloat16)
    weights = jnp.where(rows_iota == first_at, w_first, zero) + jnp.where(
        rows_iota == second_at, w_second, zero
    )
    delta = jnp.einsum(
        "tkmi,tkip->tkmp", tile_values, weights, preferred_element_type=jnp.float32
    )
    post = mon_real[:, None, :, None] + delta
    loading = jnp.sqrt(post * post + react_sq[:, None, :, None]) / mon_limit[:, None, :, None]
    neg = jnp.float32(-jnp.inf)
    loading = jnp.where(valid[:, :, None, None], loading, neg)

    base_load = jnp.sqrt(mon_real * mon_real + react_sq) / mon_limit
    block_iota = jnp.arange(blocks, dtype=jnp.int32)
    matches = tile_ids[:, :, None] == block_iota[None, None, :]
    absent = jnp.logical_not(jnp.any(matches, axis=1))
    any_absent = jnp.any(absent, axis=1)

    peak_load = jnp.max(loading, axis=(1, 3))
    peak_load = jnp.maximum(peak_load, jnp.where(any_absent[:, None], base_load, neg))

    col_max = jnp.max(loading, axis=2)
    worst_local = jnp.max(
        jnp.where(matches[:, :, :, None], col_max[:, :, None, :], neg), axis=(0, 1)
    )
    base_max = jnp.max(base_load, axis=1)
    absent_max = jnp.max(jnp.where(absent, base_max[:, None], neg), axis=0)
    worst_local = jnp.maximum(worst_local, absent_max[:, None])

    worst_own = scatter_max(worst_local.reshape(blocks * halves, half_width), both)[None, :]
    return (peak_load.reshape(-1), worst_own)


def solution(mesh):
    return jax.shard_map(
        body,
        mesh=mesh,
        in_specs=(
            P(("cases", "blk", "state")),
            P(("cases", "blk", "state")),
            P(("cases", "blk", "state")),
            P(("cases", "blk", "state")),
            P(("cases", "blk", "state")),
            P(("cases", "blk", "state"), None),
            P(("cases", "blk", "state"), None, None, None),
            P(("cases", "blk"), None),
            P(("cases", "blk"), None, None),
            P(("cases", "blk"), None, None),
        ),
        out_specs=(P(("cases", "blk", "state")), P(("cases", "blk"), "state")),
        check_vma=False,
    )
```

```python
import jax
import jax.numpy as jnp
from jax import lax
from jax.sharding import PartitionSpec as P


def axes_size(axes):
    size = 1
    for axis in axes:
        size *= lax.axis_size(axis)
    return size


def gather_doubling(x, axes):
    n = axes_size(axes)
    me = lax.axis_index(axes)
    cur = x[None]
    bit = 1
    while bit < n:
        other = lax.ppermute(cur, axes, [(j, j ^ bit) for j in range(n)])
        low = (me & bit) == 0
        cur = jnp.where(low, jnp.concatenate([cur, other]), jnp.concatenate([other, cur]))
        bit *= 2
    return cur


def scatter_max(x, axes):
    n = axes_size(axes)
    me = lax.axis_index(axes)
    cur = x
    bit = 1
    while bit < n:
        pairs = cur.reshape((cur.shape[0] // 2, 2) + cur.shape[1:])
        mine = (me // bit) % 2
        keep = lax.dynamic_index_in_dim(pairs, mine, 1, keepdims=False)
        send = lax.dynamic_index_in_dim(pairs, 1 - mine, 1, keepdims=False)
        cur = jnp.maximum(keep, lax.ppermute(send, axes, [(j, j ^ bit) for j in range(n)]))
        bit *= 2
    return cur[0]


def body(
    base_real,
    base_reactive,
    voltage,
    rating,
    monitored,
    tile_ids,
    tile_values,
    outage_ids,
    coupling,
    outage_pairs,
):
    tiles_dev, slot_count, tile_size, _ = tile_values.shape
    pair_count = outage_pairs.shape[2]
    blocks = lax.axis_size("blk")
    halves = lax.axis_size("state")
    half_width = pair_count // halves
    half_len = base_real.shape[0]
    me_state = lax.axis_index("state")
    both = ("blk", "state")

    first_idx = outage_pairs[0, 0]
    second_idx = outage_pairs[0, 1]
    local_at = outage_ids[0] - me_state * half_len
    branch_iota = lax.broadcasted_iota(jnp.int32, (pair_count, half_len), 1)
    pick_branch = (branch_iota == local_at[:, None]).astype(jnp.bfloat16)
    flow_part = jnp.dot(
        pick_branch, base_real.astype(jnp.bfloat16), preferred_element_type=jnp.float32
    )
    pair_at = jnp.concatenate([first_idx, second_idx])
    pair_to = jnp.concatenate([second_idx, first_idx])
    outage_iota = lax.broadcasted_iota(jnp.int32, (2 * pair_count, pair_count), 1)
    pick_at = (outage_iota == pair_at[:, None]).astype(jnp.bfloat16)
    flow_pairs = jnp.dot(
        pick_at, flow_part.astype(jnp.bfloat16), preferred_element_type=jnp.float32
    ).reshape(2, pair_count)
    coupled_rows = jnp.dot(pick_at, coupling[0], preferred_element_type=jnp.float32)
    coupled = jnp.sum(
        jnp.where(outage_iota == pair_to[:, None], coupled_rows, 0.0), axis=1
    ).reshape(2, pair_count)
    packed = jnp.concatenate(
        [flow_pairs, coupled, outage_pairs[0].astype(jnp.float32)]
    )
    known = gather_doubling(packed, both).reshape(blocks, halves, 6, pair_count)

    state_local = jnp.stack(
        [base_real, base_reactive * base_reactive, voltage * rating], axis=1
    )
    other_half = lax.ppermute(
        state_local, "state", [(j, (j + 1) % halves) for j in range(halves)]
    )
    state_pos = jnp.concatenate([state_local, other_half])
    mon_at = (monitored - me_state * half_len) % (halves * half_len)
    mon_vals = jnp.take(state_pos, mon_at, axis=0, mode="clip")
    mon_real = mon_vals[:, 0].reshape(tiles_dev, tile_size)
    react_sq = mon_vals[:, 1].reshape(tiles_dev, tile_size)
    mon_limit = mon_vals[:, 2].reshape(tiles_dev, tile_size)

    flow_first = jnp.sum(known[:, :, 0], axis=1)
    flow_second = jnp.sum(known[:, :, 1], axis=1)
    s_first_second = known[:, 0, 2]
    s_second_first = known[:, 0, 3]
    determinant = 1.0 - s_first_second * s_second_first
    w_first_all = (flow_first + s_first_second * flow_second) / determinant
    w_second_all = (flow_second + s_second_first * flow_first) / determinant
    table = jnp.stack([w_first_all, w_second_all, known[:, 0, 4], known[:, 0, 5]], axis=1)

    valid = tile_ids >= 0
    block_of = jnp.clip(tile_ids, 0, blocks - 1)
    chosen = jnp.take(table, block_of, axis=0)
    rows_iota = lax.broadcasted_iota(jnp.int32, (1, 1, tile_size, pair_count), 2)
    first_at = chosen[:, :, 2].astype(jnp.int32)[:, :, None, :]
    second_at = chosen[:, :, 3].astype(jnp.int32)[:, :, None, :]
    w_first = chosen[:, :, 0].astype(jnp.bfloat16)[:, :, None, :]
    w_second = chosen[:, :, 1].astype(jnp.bfloat16)[:, :, None, :]
    zero = jnp.zeros((), jnp.bfloat16)
    weights = jnp.where(rows_iota == first_at, w_first, zero) + jnp.where(
        rows_iota == second_at, w_second, zero
    )
    delta = jnp.einsum(
        "tkmi,tkip->tkmp", tile_values, weights, preferred_element_type=jnp.float32
    )
    inv_limit_sq = 1.0 / (mon_limit * mon_limit)
    post = mon_real[:, None, :, None] + delta
    squared = (post * post + react_sq[:, None, :, None]) * inv_limit_sq[:, None, :, None]
    neg = jnp.float32(-jnp.inf)
    squared = jnp.where(valid[:, :, None, None], squared, neg)

    base_sq = (mon_real * mon_real + react_sq) * inv_limit_sq
    block_iota = jnp.arange(blocks, dtype=jnp.int32)
    matches = tile_ids[:, :, None] == block_iota[None, None, :]
    absent = jnp.logical_not(jnp.any(matches, axis=1))
    any_absent = jnp.any(absent, axis=1)

    peak_sq = jnp.max(squared, axis=(1, 3))
    peak_sq = jnp.maximum(peak_sq, jnp.where(any_absent[:, None], base_sq, neg))
    peak_load = jnp.sqrt(peak_sq)

    col_max = jnp.max(squared, axis=2)
    worst_local = jnp.max(
        jnp.where(matches[:, :, :, None], col_max[:, :, None, :], neg), axis=(0, 1)
    )
    base_max = jnp.max(base_sq, axis=1)
    absent_max = jnp.max(jnp.where(absent, base_max[:, None], neg), axis=0)
    worst_local = jnp.maximum(worst_local, absent_max[:, None])

    worst_sq = scatter_max(worst_local.reshape(blocks * halves, half_width), both)
    worst_own = jnp.sqrt(worst_sq)[None, :]
    return (peak_load.reshape(-1), worst_own)


def solution(mesh):
    return jax.shard_map(
        body,
        mesh=mesh,
        in_specs=(
            P(("cases", "blk", "state")),
            P(("cases", "blk", "state")),
            P(("cases", "blk", "state")),
            P(("cases", "blk", "state")),
            P(("cases", "blk", "state")),
            P(("cases", "blk", "state"), None),
            P(("cases", "blk", "state"), None, None, None),
            P(("cases", "blk"), None),
            P(("cases", "blk"), None, None),
            P(("cases", "blk"), None, None),
        ),
        out_specs=(P(("cases", "blk", "state")), P(("cases", "blk"), "state")),
        check_vma=False,
    )
```

```python
import jax
import jax.numpy as jnp
from jax import lax
from jax.sharding import PartitionSpec as P


def axes_size(axes):
    size = 1
    for axis in axes:
        size *= lax.axis_size(axis)
    return size


def gather_doubling(x, axes):
    n = axes_size(axes)
    me = lax.axis_index(axes)
    cur = x[None]
    bit = 1
    while bit < n:
        other = lax.ppermute(cur, axes, [(j, j ^ bit) for j in range(n)])
        low = (me & bit) == 0
        cur = jnp.where(low, jnp.concatenate([cur, other]), jnp.concatenate([other, cur]))
        bit *= 2
    return cur


def scatter_max(x, axes):
    n = axes_size(axes)
    me = lax.axis_index(axes)
    cur = x
    bit = 1
    while bit < n:
        pairs = cur.reshape((cur.shape[0] // 2, 2) + cur.shape[1:])
        mine = (me // bit) % 2
        keep = lax.dynamic_index_in_dim(pairs, mine, 1, keepdims=False)
        send = lax.dynamic_index_in_dim(pairs, 1 - mine, 1, keepdims=False)
        cur = jnp.maximum(keep, lax.ppermute(send, axes, [(j, j ^ bit) for j in range(n)]))
        bit *= 2
    return cur[0]


def body(
    base_real,
    base_reactive,
    voltage,
    rating,
    monitored,
    tile_ids,
    tile_values,
    outage_ids,
    coupling,
    outage_pairs,
):
    tiles_dev, slot_count, tile_size, _ = tile_values.shape
    pair_count = outage_pairs.shape[2]
    blocks = lax.axis_size("blk")
    halves = lax.axis_size("state")
    half_width = pair_count // halves
    half_len = base_real.shape[0]
    me_state = lax.axis_index("state")
    both = ("blk", "state")

    first_idx = outage_pairs[0, 0]
    second_idx = outage_pairs[0, 1]
    local_at = outage_ids[0] - me_state * half_len
    branch_iota = lax.broadcasted_iota(jnp.int32, (pair_count, half_len), 1)
    pick_branch = (branch_iota == local_at[:, None]).astype(jnp.bfloat16)
    flow_part = jnp.dot(
        pick_branch, base_real.astype(jnp.bfloat16), preferred_element_type=jnp.float32
    )
    pair_at = jnp.concatenate([first_idx, second_idx])
    pair_to = jnp.concatenate([second_idx, first_idx])
    outage_iota = lax.broadcasted_iota(jnp.int32, (2 * pair_count, pair_count), 1)
    pick_at = (outage_iota == pair_at[:, None]).astype(jnp.bfloat16)
    flow_pairs = jnp.dot(
        pick_at, flow_part.astype(jnp.bfloat16), preferred_element_type=jnp.float32
    ).reshape(2, pair_count)
    flow_other = lax.ppermute(
        flow_pairs, "state", [(j, (j + 1) % halves) for j in range(halves)]
    )
    coupled_rows = jnp.dot(pick_at, coupling[0], preferred_element_type=jnp.float32)
    coupled = jnp.sum(
        jnp.where(outage_iota == pair_to[:, None], coupled_rows, 0.0), axis=1
    ).reshape(2, pair_count)
    flows = flow_pairs + flow_other
    determinant = 1.0 - coupled[0] * coupled[1]
    w_first = (flows[0] + coupled[0] * flows[1]) / determinant
    w_second = (flows[1] + coupled[1] * flows[0]) / determinant
    packed = jnp.stack([w_first, w_second, first_idx.astype(jnp.float32), second_idx.astype(jnp.float32)])
    table = gather_doubling(packed.astype(jnp.bfloat16), ("blk",))

    state_local = jnp.stack(
        [base_real, base_reactive * base_reactive, voltage * rating], axis=1
    )
    other_half = lax.ppermute(
        state_local, "state", [(j, (j + 1) % halves) for j in range(halves)]
    )
    state_pos = jnp.concatenate([state_local, other_half])
    mon_at = (monitored - me_state * half_len) % (halves * half_len)
    mon_vals = jnp.take(state_pos, mon_at, axis=0, mode="clip")
    mon_real = mon_vals[:, 0].reshape(tiles_dev, tile_size)
    react_sq = mon_vals[:, 1].reshape(tiles_dev, tile_size)
    mon_limit = mon_vals[:, 2].reshape(tiles_dev, tile_size)

    valid = tile_ids >= 0
    block_of = jnp.clip(tile_ids, 0, blocks - 1)
    chosen = jnp.take(table, block_of, axis=0)
    rows_iota = lax.broadcasted_iota(jnp.int32, (1, 1, tile_size, pair_count), 2)
    first_at = chosen[:, :, 2].astype(jnp.int32)[:, :, None, :]
    second_at = chosen[:, :, 3].astype(jnp.int32)[:, :, None, :]
    w_first = chosen[:, :, 0][:, :, None, :]
    w_second = chosen[:, :, 1][:, :, None, :]
    zero = jnp.zeros((), jnp.bfloat16)
    weights = jnp.where(rows_iota == first_at, w_first, zero) + jnp.where(
        rows_iota == second_at, w_second, zero
    )
    delta = jnp.einsum(
        "tkmi,tkip->tkmp", tile_values, weights, preferred_element_type=jnp.float32
    )
    inv_limit_sq = 1.0 / (mon_limit * mon_limit)
    post = mon_real[:, None, :, None] + delta
    squared = (post * post + react_sq[:, None, :, None]) * inv_limit_sq[:, None, :, None]
    neg = jnp.float32(-jnp.inf)
    squared = jnp.where(valid[:, :, None, None], squared, neg)

    base_sq = (mon_real * mon_real + react_sq) * inv_limit_sq
    block_iota = jnp.arange(blocks, dtype=jnp.int32)
    matches = tile_ids[:, :, None] == block_iota[None, None, :]
    absent = jnp.logical_not(jnp.any(matches, axis=1))
    any_absent = jnp.any(absent, axis=1)

    peak_sq = jnp.max(squared, axis=(1, 3))
    peak_sq = jnp.maximum(peak_sq, jnp.where(any_absent[:, None], base_sq, neg))
    peak_load = jnp.sqrt(peak_sq)

    col_max = jnp.max(squared, axis=2)
    worst_local = jnp.max(
        jnp.where(matches[:, :, :, None], col_max[:, :, None, :], neg), axis=(0, 1)
    )
    base_max = jnp.max(base_sq, axis=1)
    absent_max = jnp.max(jnp.where(absent, base_max[:, None], neg), axis=0)
    worst_local = jnp.maximum(worst_local, absent_max[:, None])

    worst_sq = scatter_max(worst_local.reshape(blocks * halves, half_width), both)
    worst_own = jnp.sqrt(worst_sq)[None, :]
    return (peak_load.reshape(-1), worst_own)


def solution(mesh):
    return jax.shard_map(
        body,
        mesh=mesh,
        in_specs=(
            P(("cases", "blk", "state")),
            P(("cases", "blk", "state")),
            P(("cases", "blk", "state")),
            P(("cases", "blk", "state")),
            P(("cases", "blk", "state")),
            P(("cases", "blk", "state"), None),
            P(("cases", "blk", "state"), None, None, None),
            P(("cases", "blk"), None),
            P(("cases", "blk"), None, None),
            P(("cases", "blk"), None, None),
        ),
        out_specs=(P(("cases", "blk", "state")), P(("cases", "blk"), "state")),
        check_vma=False,
    )
```

```python
import jax
import jax.numpy as jnp
from jax import lax
from jax.sharding import PartitionSpec as P


def axes_size(axes):
    size = 1
    for axis in axes:
        size *= lax.axis_size(axis)
    return size


def gather_doubling(x, axes):
    n = axes_size(axes)
    me = lax.axis_index(axes)
    cur = x[None]
    bit = 1
    while bit < n:
        other = lax.ppermute(cur, axes, [(j, j ^ bit) for j in range(n)])
        low = (me & bit) == 0
        cur = jnp.where(low, jnp.concatenate([cur, other]), jnp.concatenate([other, cur]))
        bit *= 2
    return cur


def scatter_max(x, axes):
    n = axes_size(axes)
    me = lax.axis_index(axes)
    cur = x
    bit = 1
    while bit < n:
        pairs = cur.reshape((cur.shape[0] // 2, 2) + cur.shape[1:])
        mine = (me // bit) % 2
        keep = lax.dynamic_index_in_dim(pairs, mine, 1, keepdims=False)
        send = lax.dynamic_index_in_dim(pairs, 1 - mine, 1, keepdims=False)
        cur = jnp.maximum(keep, lax.ppermute(send, axes, [(j, j ^ bit) for j in range(n)]))
        bit *= 2
    return cur[0]


def body(
    base_real,
    base_reactive,
    voltage,
    rating,
    monitored,
    tile_ids,
    tile_values,
    outage_ids,
    coupling,
    outage_pairs,
):
    tiles_dev, _, tile_size, _ = tile_values.shape
    pair_count = outage_pairs.shape[2]
    blocks = lax.axis_size("blk")
    halves = lax.axis_size("state")
    half_width = pair_count // halves
    half_len = base_real.shape[0]
    me_state = lax.axis_index("state")
    both = ("blk", "state")

    first_idx = outage_pairs[0, 0]
    second_idx = outage_pairs[0, 1]
    local_at = outage_ids[0] - me_state * half_len
    branch_iota = lax.broadcasted_iota(jnp.int32, (pair_count, half_len), 1)
    pick_branch = (branch_iota == local_at[:, None]).astype(jnp.bfloat16)
    flow_part = jnp.dot(
        pick_branch, base_real.astype(jnp.bfloat16), preferred_element_type=jnp.float32
    )
    pair_at = jnp.concatenate([first_idx, second_idx])
    pair_to = jnp.concatenate([second_idx, first_idx])
    outage_iota = lax.broadcasted_iota(jnp.int32, (2 * pair_count, pair_count), 1)
    pick_at = (outage_iota == pair_at[:, None]).astype(jnp.bfloat16)
    flow_pairs = jnp.dot(
        pick_at, flow_part.astype(jnp.bfloat16), preferred_element_type=jnp.float32
    ).reshape(2, pair_count)
    flow_other = lax.ppermute(
        flow_pairs, "state", [(j, (j + 1) % halves) for j in range(halves)]
    )
    coupled_rows = jnp.dot(pick_at, coupling[0], preferred_element_type=jnp.float32)
    coupled = jnp.sum(
        jnp.where(outage_iota == pair_to[:, None], coupled_rows, 0.0), axis=1
    ).reshape(2, pair_count)
    flows = flow_pairs + flow_other
    determinant = 1.0 - coupled[0] * coupled[1]
    w_first = (flows[0] + coupled[0] * flows[1]) / determinant
    w_second = (flows[1] + coupled[1] * flows[0]) / determinant
    packed = jnp.stack([w_first, w_second, first_idx.astype(jnp.float32), second_idx.astype(jnp.float32)])
    table = gather_doubling(packed.astype(jnp.bfloat16), ("blk",))

    state_local = jnp.stack([base_real, base_reactive * base_reactive, voltage * rating], axis=1)
    other_half = lax.ppermute(state_local, "state", [(j, (j + 1) % halves) for j in range(halves)])
    state_pos = jnp.concatenate([state_local, other_half])
    mon_at = (monitored - me_state * half_len) % (halves * half_len)
    mon_vals = jnp.take(state_pos, mon_at, axis=0, mode="clip")
    mon_real = mon_vals[:, 0].reshape(tiles_dev, tile_size)
    react_sq = mon_vals[:, 1].reshape(tiles_dev, tile_size)
    mon_limit = mon_vals[:, 2].reshape(tiles_dev, tile_size)
    inv_limit_sq = 1.0 / (mon_limit * mon_limit)
    base_sq = (mon_real * mon_real + react_sq) * inv_limit_sq

    valid = tile_ids >= 0
    block_of = jnp.clip(tile_ids, 0, blocks - 1)
    chosen = jnp.take(table, block_of, axis=0)
    rows_iota = lax.broadcasted_iota(jnp.int32, (1, 1, tile_size, pair_count), 2)
    first_at = chosen[:, :, 2].astype(jnp.int32)[:, :, None, :]
    second_at = chosen[:, :, 3].astype(jnp.int32)[:, :, None, :]
    w_first = chosen[:, :, 0][:, :, None, :]
    w_second = chosen[:, :, 1][:, :, None, :]
    zero = jnp.zeros((), jnp.bfloat16)
    weights = jnp.where(rows_iota == first_at, w_first, zero) + jnp.where(
        rows_iota == second_at, w_second, zero
    )
    delta = jnp.einsum(
        "tkmi,tkip->tkmp", tile_values, weights, preferred_element_type=jnp.float32
    )
    post = mon_real[:, None, :, None] + delta
    squared = (post * post + react_sq[:, None, :, None]) * inv_limit_sq[:, None, :, None]
    neg = jnp.float32(-jnp.inf)
    squared = jnp.where(valid[:, :, None, None], squared, neg)

    block_iota = jnp.arange(blocks, dtype=jnp.int32)
    matches = tile_ids[:, :, None] == block_iota[None, None, :]
    absent = jnp.logical_not(jnp.any(matches, axis=1))
    any_absent = jnp.any(absent, axis=1)

    peak_sq = jnp.max(squared, axis=(1, 3))
    peak_sq = jnp.maximum(peak_sq, jnp.where(any_absent[:, None], base_sq, neg))
    peak_load = jnp.sqrt(peak_sq)

    col_max = jnp.max(squared, axis=2)
    worst_local = jnp.max(
        jnp.where(matches[:, :, :, None], col_max[:, :, None, :], neg), axis=(0, 1)
    )
    base_max = jnp.max(base_sq, axis=1)
    absent_max = jnp.max(jnp.where(absent, base_max[:, None], neg), axis=0)
    worst_local = jnp.maximum(worst_local, absent_max[:, None])

    worst_sq = scatter_max(worst_local.reshape(blocks * halves, half_width), both)
    worst_own = jnp.sqrt(worst_sq)[None, :]
    return (peak_load.reshape(-1), worst_own)


def solution(mesh):
    return jax.shard_map(
        body,
        mesh=mesh,
        in_specs=(
            P(("cases", "blk", "state")),
            P(("cases", "blk", "state")),
            P(("cases", "blk", "state")),
            P(("cases", "blk", "state")),
            P(("cases", "blk", "state")),
            P(("cases", "blk", "state"), None),
            P(("cases", "blk", "state"), None, None, None),
            P(("cases", "blk"), None),
            P(("cases", "blk"), None, None),
            P(("cases", "blk"), None, None),
        ),
        out_specs=(P(("cases", "blk", "state")), P(("cases", "blk"), "state")),
        check_vma=False,
    )
```

```python
import jax
import jax.numpy as jnp
from jax import lax
from jax.experimental import pallas as pl
from jax.experimental.pallas import tpu as pltpu
from jax.sharding import PartitionSpec as P


def axes_size(axes):
    size = 1
    for axis in axes:
        size *= lax.axis_size(axis)
    return size


def gather_doubling(x, axes):
    n = axes_size(axes)
    me = lax.axis_index(axes)
    cur = x[None]
    bit = 1
    while bit < n:
        other = lax.ppermute(cur, axes, [(j, j ^ bit) for j in range(n)])
        low = (me & bit) == 0
        cur = jnp.where(low, jnp.concatenate([cur, other]), jnp.concatenate([other, cur]))
        bit *= 2
    return cur


def scatter_max(x, axes):
    n = axes_size(axes)
    me = lax.axis_index(axes)
    cur = x
    bit = 1
    while bit < n:
        pairs = cur.reshape((cur.shape[0] // 2, 2) + cur.shape[1:])
        mine = (me // bit) % 2
        keep = lax.dynamic_index_in_dim(pairs, mine, 1, keepdims=False)
        send = lax.dynamic_index_in_dim(pairs, 1 - mine, 1, keepdims=False)
        cur = jnp.maximum(keep, lax.ppermute(send, axes, [(j, j ^ bit) for j in range(n)]))
        bit *= 2
    return cur[0]


def prep_kernel(me_ref, real_ref, ids_ref, pairs_ref, coupling_ref, flow_ref, coupled_ref):
    half_len = real_ref.shape[1]
    outages = ids_ref.shape[1]
    local_at = ids_ref[...] - me_ref[0] * half_len
    branch_iota = lax.broadcasted_iota(jnp.int32, (half_len, outages), 0)
    pick_branch = (branch_iota == local_at).astype(jnp.bfloat16)
    real = real_ref[...].astype(jnp.bfloat16)
    flow_part = jnp.dot(real, pick_branch, preferred_element_type=jnp.float32)
    pairs = pairs_ref[0]
    pair_at = jnp.concatenate([pairs[0:1], pairs[1:2]], axis=1)
    pair_to = jnp.concatenate([pairs[1:2], pairs[0:1]], axis=1)
    outage_iota = lax.broadcasted_iota(jnp.int32, (outages, pair_at.shape[1]), 0)
    pick_at = (outage_iota == pair_at).astype(jnp.bfloat16)
    flow_ref[...] = jnp.dot(
        flow_part.astype(jnp.bfloat16), pick_at, preferred_element_type=jnp.float32
    )
    columns = jnp.dot(coupling_ref[0], pick_at, preferred_element_type=jnp.float32)
    rows = (outage_iota == pair_to).astype(jnp.float32)
    coupled_ref[...] = jnp.sum(columns * rows, axis=0, keepdims=True)


def prep_call(me_state, base_real, outage_ids, outage_pairs, coupling):
    pair_count = outage_pairs.shape[2]
    vmem = pl.BlockSpec(memory_space=pltpu.VMEM)
    flow, coupled = pl.pallas_call(
        prep_kernel,
        out_shape=(
            jax.ShapeDtypeStruct((1, 2 * pair_count), jnp.float32),
            jax.ShapeDtypeStruct((1, 2 * pair_count), jnp.float32),
        ),
        in_specs=[pl.BlockSpec(memory_space=pltpu.SMEM), vmem, vmem, vmem, vmem],
        out_specs=(vmem, vmem),
    )(me_state.reshape(1), base_real.reshape(1, -1), outage_ids, outage_pairs, coupling)
    return flow.reshape(2, pair_count), coupled.reshape(2, pair_count)[::-1]


def body(
    base_real,
    base_reactive,
    voltage,
    rating,
    monitored,
    tile_ids,
    tile_values,
    outage_ids,
    coupling,
    outage_pairs,
):
    tiles_dev, slot_count, tile_size, _ = tile_values.shape
    pair_count = outage_pairs.shape[2]
    blocks = lax.axis_size("blk")
    halves = lax.axis_size("state")
    half_width = pair_count // halves
    half_len = base_real.shape[0]
    me_state = lax.axis_index("state")
    both = ("blk", "state")

    first_idx = outage_pairs[0, 0]
    second_idx = outage_pairs[0, 1]
    flow_pairs, coupled = prep_call(me_state, base_real, outage_ids, outage_pairs, coupling)
    flow_other = lax.ppermute(
        flow_pairs, "state", [(j, (j + 1) % halves) for j in range(halves)]
    )
    flows = flow_pairs + flow_other
    determinant = 1.0 - coupled[0] * coupled[1]
    w_first = (flows[0] + coupled[0] * flows[1]) / determinant
    w_second = (flows[1] + coupled[1] * flows[0]) / determinant
    packed = jnp.stack([w_first, w_second, first_idx.astype(jnp.float32), second_idx.astype(jnp.float32)])
    table = gather_doubling(packed.astype(jnp.bfloat16), ("blk",))

    state_local = jnp.stack(
        [base_real, base_reactive * base_reactive, voltage * rating], axis=1
    )
    other_half = lax.ppermute(
        state_local, "state", [(j, (j + 1) % halves) for j in range(halves)]
    )
    state_pos = jnp.concatenate([state_local, other_half])
    mon_at = (monitored - me_state * half_len) % (halves * half_len)
    mon_vals = jnp.take(state_pos, mon_at, axis=0, mode="clip")
    mon_real = mon_vals[:, 0].reshape(tiles_dev, tile_size)
    react_sq = mon_vals[:, 1].reshape(tiles_dev, tile_size)
    mon_limit = mon_vals[:, 2].reshape(tiles_dev, tile_size)
    inv_limit_sq = 1.0 / (mon_limit * mon_limit)
    base_sq = (mon_real * mon_real + react_sq) * inv_limit_sq

    valid = tile_ids >= 0
    block_of = jnp.clip(tile_ids, 0, blocks - 1)
    pick_block = (block_of.reshape(-1, 1) == jnp.arange(blocks, dtype=jnp.int32)[None, :]).astype(jnp.bfloat16)
    chosen = jnp.dot(pick_block, table.reshape(blocks, -1), preferred_element_type=jnp.float32)
    chosen = chosen.astype(jnp.bfloat16).reshape(tiles_dev, slot_count, 4, pair_count)
    rows_iota = lax.broadcasted_iota(jnp.int32, (1, 1, tile_size, pair_count), 2)
    first_at = chosen[:, :, 2].astype(jnp.int32)[:, :, None, :]
    second_at = chosen[:, :, 3].astype(jnp.int32)[:, :, None, :]
    w_first = chosen[:, :, 0][:, :, None, :]
    w_second = chosen[:, :, 1][:, :, None, :]
    zero = jnp.zeros((), jnp.bfloat16)
    weights = jnp.where(rows_iota == first_at, w_first, zero) + jnp.where(
        rows_iota == second_at, w_second, zero
    )
    delta = jnp.einsum(
        "tkmi,tkip->tkmp", tile_values, weights, preferred_element_type=jnp.float32
    )
    post = mon_real[:, None, :, None] + delta
    squared = (post * post + react_sq[:, None, :, None]) * inv_limit_sq[:, None, :, None]
    neg = jnp.float32(-jnp.inf)
    squared = jnp.where(valid[:, :, None, None], squared, neg)

    block_iota = jnp.arange(blocks, dtype=jnp.int32)
    matches = tile_ids[:, :, None] == block_iota[None, None, :]
    absent = jnp.logical_not(jnp.any(matches, axis=1))
    any_absent = jnp.any(absent, axis=1)

    peak_sq = jnp.max(squared, axis=(1, 3))
    peak_sq = jnp.maximum(peak_sq, jnp.where(any_absent[:, None], base_sq, neg))
    peak_load = jnp.sqrt(peak_sq)

    col_max = jnp.max(squared, axis=2)
    worst_local = jnp.max(
        jnp.where(matches[:, :, :, None], col_max[:, :, None, :], neg), axis=(0, 1)
    )
    base_max = jnp.max(base_sq, axis=1)
    absent_max = jnp.max(jnp.where(absent, base_max[:, None], neg), axis=0)
    worst_local = jnp.maximum(worst_local, absent_max[:, None])

    worst_sq = scatter_max(worst_local.reshape(blocks * halves, half_width), both)
    worst_own = jnp.sqrt(worst_sq)[None, :]
    return (peak_load.reshape(-1), worst_own)


def solution(mesh):
    return jax.shard_map(
        body,
        mesh=mesh,
        in_specs=(
            P(("cases", "blk", "state")),
            P(("cases", "blk", "state")),
            P(("cases", "blk", "state")),
            P(("cases", "blk", "state")),
            P(("cases", "blk", "state")),
            P(("cases", "blk", "state"), None),
            P(("cases", "blk", "state"), None, None, None),
            P(("cases", "blk"), None),
            P(("cases", "blk"), None, None),
            P(("cases", "blk"), None, None),
        ),
        out_specs=(P(("cases", "blk", "state")), P(("cases", "blk"), "state")),
        check_vma=False,
    )
```

```python
import jax
import jax.numpy as jnp
from jax import lax
from jax.sharding import PartitionSpec as P


def axes_size(axes):
    size = 1
    for axis in axes:
        size *= lax.axis_size(axis)
    return size


def gather_doubling(x, axes):
    n = axes_size(axes)
    me = lax.axis_index(axes)
    cur = x[None]
    bit = 1
    while bit < n:
        other = lax.ppermute(cur, axes, [(j, j ^ bit) for j in range(n)])
        low = (me & bit) == 0
        cur = jnp.where(low, jnp.concatenate([cur, other]), jnp.concatenate([other, cur]))
        bit *= 2
    return cur


def scatter_max(x, axes):
    n = axes_size(axes)
    me = lax.axis_index(axes)
    cur = x
    bit = 1
    while bit < n:
        pairs = cur.reshape((cur.shape[0] // 2, 2) + cur.shape[1:])
        mine = (me // bit) % 2
        keep = lax.dynamic_index_in_dim(pairs, mine, 1, keepdims=False)
        send = lax.dynamic_index_in_dim(pairs, 1 - mine, 1, keepdims=False)
        cur = jnp.maximum(keep, lax.ppermute(send, axes, [(j, j ^ bit) for j in range(n)]))
        bit *= 2
    return cur[0]


def body(
    base_real,
    base_reactive,
    voltage,
    rating,
    monitored,
    tile_ids,
    tile_values,
    outage_ids,
    coupling,
    outage_pairs,
):
    tiles_dev, slot_count, tile_size, _ = tile_values.shape
    pair_count = outage_pairs.shape[2]
    blocks = lax.axis_size("blk")
    halves = lax.axis_size("state")
    half_width = pair_count // halves
    half_len = base_real.shape[0]
    me_state = lax.axis_index("state")
    both = ("blk", "state")

    first_idx = outage_pairs[0, 0]
    second_idx = outage_pairs[0, 1]
    local_at = outage_ids[0] - me_state * half_len
    branch_iota = lax.broadcasted_iota(jnp.int32, (pair_count, half_len), 1)
    pick_branch = (branch_iota == local_at[:, None]).astype(jnp.bfloat16)
    flow_part = jnp.dot(
        pick_branch, base_real.astype(jnp.bfloat16), preferred_element_type=jnp.float32
    )
    pair_at = jnp.concatenate([first_idx, second_idx])
    pair_to = jnp.concatenate([second_idx, first_idx])
    outage_iota = lax.broadcasted_iota(jnp.int32, (2 * pair_count, pair_count), 1)
    pick_at = (outage_iota == pair_at[:, None]).astype(jnp.bfloat16)
    flow_pairs = jnp.dot(
        pick_at, flow_part.astype(jnp.bfloat16), preferred_element_type=jnp.float32
    ).reshape(2, pair_count)
    flow_other = lax.ppermute(
        flow_pairs, "state", [(j, (j + 1) % halves) for j in range(halves)]
    )
    coupled_rows = jnp.dot(pick_at, coupling[0], preferred_element_type=jnp.float32)
    coupled = jnp.sum(
        jnp.where(outage_iota == pair_to[:, None], coupled_rows, 0.0), axis=1
    ).reshape(2, pair_count)
    flows = flow_pairs + flow_other
    determinant = 1.0 - coupled[0] * coupled[1]
    w_first = (flows[0] + coupled[0] * flows[1]) / determinant
    w_second = (flows[1] + coupled[1] * flows[0]) / determinant
    packed = jnp.stack([w_first, w_second, first_idx.astype(jnp.float32), second_idx.astype(jnp.float32)])
    table = gather_doubling(packed.astype(jnp.bfloat16), ("blk",))

    state_local = jnp.stack([base_real, base_reactive * base_reactive, voltage * rating], axis=1)
    other_half = lax.ppermute(state_local, "state", [(j, (j + 1) % halves) for j in range(halves)])
    state_pos = jnp.concatenate([state_local, other_half])
    mon_at = (monitored - me_state * half_len) % (halves * half_len)
    mon_vals = jnp.take(state_pos, mon_at, axis=0, mode="clip")
    mon_real = mon_vals[:, 0].reshape(tiles_dev, tile_size)
    react_sq = mon_vals[:, 1].reshape(tiles_dev, tile_size)
    mon_limit = mon_vals[:, 2].reshape(tiles_dev, tile_size)
    inv_limit_sq = 1.0 / (mon_limit * mon_limit)
    base_sq = (mon_real * mon_real + react_sq) * inv_limit_sq

    valid = tile_ids >= 0
    block_of = jnp.clip(tile_ids, 0, blocks - 1)
    pick_block = (block_of.reshape(-1, 1) == jnp.arange(blocks, dtype=jnp.int32)[None, :]).astype(jnp.bfloat16)
    chosen = jnp.dot(pick_block, table.reshape(blocks, -1), preferred_element_type=jnp.float32)
    chosen = chosen.astype(jnp.bfloat16).reshape(tiles_dev, slot_count, 4, pair_count)
    rows_iota = lax.broadcasted_iota(jnp.int32, (1, 1, tile_size, pair_count), 2)
    first_at = chosen[:, :, 2].astype(jnp.int32)[:, :, None, :]
    second_at = chosen[:, :, 3].astype(jnp.int32)[:, :, None, :]
    w_first = chosen[:, :, 0][:, :, None, :]
    w_second = chosen[:, :, 1][:, :, None, :]
    zero = jnp.zeros((), jnp.bfloat16)
    weights = jnp.where(rows_iota == first_at, w_first, zero) + jnp.where(
        rows_iota == second_at, w_second, zero
    )
    delta = jnp.einsum(
        "tkmi,tkip->tkmp", tile_values, weights, preferred_element_type=jnp.float32
    )
    post = mon_real[:, None, :, None] + delta
    squared = (post * post + react_sq[:, None, :, None]) * inv_limit_sq[:, None, :, None]
    neg = jnp.float32(-jnp.inf)
    squared = jnp.where(valid[:, :, None, None], squared, neg)

    block_iota = jnp.arange(blocks, dtype=jnp.int32)
    matches = tile_ids[:, :, None] == block_iota[None, None, :]
    absent = jnp.logical_not(jnp.any(matches, axis=1))
    any_absent = jnp.any(absent, axis=1)

    peak_sq = jnp.max(squared, axis=(1, 3))
    peak_sq = jnp.maximum(peak_sq, jnp.where(any_absent[:, None], base_sq, neg))
    peak_load = jnp.sqrt(peak_sq)

    col_max = jnp.max(squared, axis=2)
    worst_local = jnp.max(
        jnp.where(matches[:, :, :, None], col_max[:, :, None, :], neg), axis=(0, 1)
    )
    base_max = jnp.max(base_sq, axis=1)
    absent_max = jnp.max(jnp.where(absent, base_max[:, None], neg), axis=0)
    worst_local = jnp.maximum(worst_local, absent_max[:, None])

    worst_sq = scatter_max(worst_local.reshape(blocks * halves, half_width), both)
    worst_own = jnp.sqrt(worst_sq)[None, :]
    return (peak_load.reshape(-1), worst_own)


def solution(mesh):
    return jax.shard_map(
        body,
        mesh=mesh,
        in_specs=(
            P(("cases", "blk", "state")),
            P(("cases", "blk", "state")),
            P(("cases", "blk", "state")),
            P(("cases", "blk", "state")),
            P(("cases", "blk", "state")),
            P(("cases", "blk", "state"), None),
            P(("cases", "blk", "state"), None, None, None),
            P(("cases", "blk"), None),
            P(("cases", "blk"), None, None),
            P(("cases", "blk"), None, None),
        ),
        out_specs=(P(("cases", "blk", "state")), P(("cases", "blk"), "state")),
        check_vma=False,
    )
```

```python
import jax
import jax.numpy as jnp
from jax import lax
from jax.sharding import PartitionSpec as P


def axes_size(axes):
    size = 1
    for axis in axes:
        size *= lax.axis_size(axis)
    return size


def gather_doubling(x, axes):
    n = axes_size(axes)
    me = lax.axis_index(axes)
    cur = x[None]
    bit = 1
    while bit < n:
        other = lax.ppermute(cur, axes, [(j, j ^ bit) for j in range(n)])
        low = (me & bit) == 0
        cur = jnp.where(low, jnp.concatenate([cur, other]), jnp.concatenate([other, cur]))
        bit *= 2
    return cur


def scatter_max(x, axes):
    n = axes_size(axes)
    me = lax.axis_index(axes)
    cur = x
    bit = 1
    while bit < n:
        pairs = cur.reshape((cur.shape[0] // 2, 2) + cur.shape[1:])
        mine = (me // bit) % 2
        keep = lax.dynamic_index_in_dim(pairs, mine, 1, keepdims=False)
        send = lax.dynamic_index_in_dim(pairs, 1 - mine, 1, keepdims=False)
        got = lax.ppermute(send, axes, [(j, j ^ bit) for j in range(n)])
        cur = jnp.maximum(keep, got)
        bit *= 2
    return cur[0]


def body(
    base_real,
    base_reactive,
    voltage,
    rating,
    monitored,
    tile_ids,
    tile_values,
    outage_ids,
    coupling,
    outage_pairs,
):
    tiles_dev, slot_count, tile_size, _ = tile_values.shape
    pair_count = outage_pairs.shape[2]
    blocks = lax.axis_size("blk")
    halves = lax.axis_size("state")
    half_width = pair_count // halves
    half_len = base_real.shape[0]
    me_state = lax.axis_index("state")
    both = ("blk", "state")

    first_idx = outage_pairs[0, 0]
    second_idx = outage_pairs[0, 1]
    local_at = outage_ids[0] - me_state * half_len
    branch_iota = lax.broadcasted_iota(jnp.int32, (pair_count, half_len), 1)
    pick_branch = (branch_iota == local_at[:, None]).astype(jnp.bfloat16)
    flow_part = jnp.dot(
        pick_branch, base_real.astype(jnp.bfloat16), preferred_element_type=jnp.float32
    )
    pair_at = jnp.concatenate([first_idx, second_idx])
    pair_to = jnp.concatenate([second_idx, first_idx])
    outage_iota = lax.broadcasted_iota(jnp.int32, (2 * pair_count, pair_count), 1)
    pick_at = (outage_iota == pair_at[:, None]).astype(jnp.bfloat16)
    flow_pairs = jnp.dot(
        pick_at, flow_part.astype(jnp.bfloat16), preferred_element_type=jnp.float32
    ).reshape(2, pair_count)
    flow_other = lax.ppermute(
        flow_pairs, "state", [(j, (j + 1) % halves) for j in range(halves)]
    )
    coupled_rows = jnp.dot(pick_at, coupling[0], preferred_element_type=jnp.float32)
    coupled = jnp.sum(
        jnp.where(outage_iota == pair_to[:, None], coupled_rows, 0.0), axis=1
    ).reshape(2, pair_count)
    flows = flow_pairs + flow_other
    determinant = 1.0 - coupled[0] * coupled[1]
    w_first = (flows[0] + coupled[0] * flows[1]) / determinant
    w_second = (flows[1] + coupled[1] * flows[0]) / determinant
    packed = jnp.stack([w_first, w_second, first_idx.astype(jnp.float32), second_idx.astype(jnp.float32)])
    table = gather_doubling(packed.astype(jnp.bfloat16), ("blk",))

    state_local = jnp.stack([base_real, base_reactive * base_reactive, voltage * rating], axis=1)
    other_half = lax.ppermute(state_local, "state", [(j, (j + 1) % halves) for j in range(halves)])
    state_pos = jnp.concatenate([state_local, other_half])
    mon_at = (monitored - me_state * half_len) % (halves * half_len)
    mon_vals = jnp.take(state_pos, mon_at, axis=0, mode="clip")
    mon_real = mon_vals[:, 0].reshape(tiles_dev, tile_size)
    react_sq = mon_vals[:, 1].reshape(tiles_dev, tile_size)
    mon_limit = mon_vals[:, 2].reshape(tiles_dev, tile_size)
    inv_limit_sq = 1.0 / (mon_limit * mon_limit)
    base_sq = (mon_real * mon_real + react_sq) * inv_limit_sq

    valid = tile_ids >= 0
    block_of = jnp.clip(tile_ids, 0, blocks - 1)
    pick_block = (block_of.reshape(-1, 1) == jnp.arange(blocks, dtype=jnp.int32)[None, :]).astype(jnp.bfloat16)
    chosen = jnp.dot(pick_block, table.reshape(blocks, -1), preferred_element_type=jnp.float32)
    chosen = chosen.astype(jnp.bfloat16).reshape(tiles_dev, slot_count, 4, pair_count)
    neg = jnp.float32(-jnp.inf)

    def slot_squares(values, rows):
        rows_iota = lax.broadcasted_iota(jnp.int32, (1, 1, tile_size, pair_count), 2)
        first_at = rows[:, :, 2].astype(jnp.int32)[:, :, None, :]
        second_at = rows[:, :, 3].astype(jnp.int32)[:, :, None, :]
        zero = jnp.zeros((), jnp.bfloat16)
        weights = jnp.where(rows_iota == first_at, rows[:, :, 0][:, :, None, :], zero) + jnp.where(
            rows_iota == second_at, rows[:, :, 1][:, :, None, :], zero
        )
        delta = jnp.einsum(
            "tkmi,tkip->tkmp", values, weights, preferred_element_type=jnp.float32
        )
        post = mon_real[:, None, :, None] + delta
        squared = (post * post + react_sq[:, None, :, None]) * inv_limit_sq[:, None, :, None]
        return jnp.where(valid[:, :, None, None], squared, neg)

    squared = slot_squares(tile_values, chosen)

    block_iota = jnp.arange(blocks, dtype=jnp.int32)
    matches = tile_ids[:, :, None] == block_iota[None, None, :]
    absent = jnp.logical_not(jnp.any(matches, axis=1))
    any_absent = jnp.any(absent, axis=1)


    col_max = jnp.max(squared, axis=2)
    worst_local = jnp.max(
        jnp.where(matches[:, :, :, None], col_max[:, :, None, :], neg), axis=(0, 1)
    )
    base_max = jnp.max(base_sq, axis=1)
    absent_max = jnp.max(jnp.where(absent, base_max[:, None], neg), axis=0)
    worst_local = jnp.maximum(worst_local, absent_max[:, None])

    worst_sq = scatter_max(worst_local.reshape(blocks * halves, half_width), both)
    worst_own = jnp.sqrt(worst_sq)[None, :]
    values_again, rows_again = lax.optimization_barrier((tile_values, chosen))
    peak_sq = jnp.max(slot_squares(values_again, rows_again), axis=(1, 3))
    peak_sq = jnp.maximum(peak_sq, jnp.where(any_absent[:, None], base_sq, neg))
    peak_load = jnp.sqrt(peak_sq)
    return (peak_load.reshape(-1), worst_own)


def solution(mesh):
    return jax.shard_map(
        body,
        mesh=mesh,
        in_specs=(
            P(("cases", "blk", "state")),
            P(("cases", "blk", "state")),
            P(("cases", "blk", "state")),
            P(("cases", "blk", "state")),
            P(("cases", "blk", "state")),
            P(("cases", "blk", "state"), None),
            P(("cases", "blk", "state"), None, None, None),
            P(("cases", "blk"), None),
            P(("cases", "blk"), None, None),
            P(("cases", "blk"), None, None),
        ),
        out_specs=(P(("cases", "blk", "state")), P(("cases", "blk"), "state")),
        check_vma=False,
    )
```

```python
import jax
import jax.numpy as jnp
from jax import lax
from jax.sharding import PartitionSpec as P


def axes_size(axes):
    size = 1
    for axis in axes:
        size *= lax.axis_size(axis)
    return size


def gather_doubling(x, axes):
    n = axes_size(axes)
    me = lax.axis_index(axes)
    cur = x[None]
    bit = 1
    while bit < n:
        other = lax.ppermute(cur, axes, [(j, j ^ bit) for j in range(n)])
        low = (me & bit) == 0
        cur = jnp.where(low, jnp.concatenate([cur, other]), jnp.concatenate([other, cur]))
        bit *= 2
    return cur


def scatter_max(x, axes):
    n = axes_size(axes)
    me = lax.axis_index(axes)
    cur = x
    bit = 1
    while bit < n:
        pairs = cur.reshape((cur.shape[0] // 2, 2) + cur.shape[1:])
        mine = (me // bit) % 2
        keep = lax.dynamic_index_in_dim(pairs, mine, 1, keepdims=False)
        send = lax.dynamic_index_in_dim(pairs, 1 - mine, 1, keepdims=False)
        got = lax.ppermute(send, axes, [(j, j ^ bit) for j in range(n)])
        cur = jnp.maximum(keep, got)
        bit *= 2
    return cur[0]


def body(
    base_real,
    base_reactive,
    voltage,
    rating,
    monitored,
    tile_ids,
    tile_values,
    outage_ids,
    coupling,
    outage_pairs,
):
    tiles_dev, _, tile_size, _ = tile_values.shape
    pair_count = outage_pairs.shape[2]
    blocks = lax.axis_size("blk")
    halves = lax.axis_size("state")
    half_width = pair_count // halves
    half_len = base_real.shape[0]
    me_state = lax.axis_index("state")
    assert halves == 2

    first_idx = outage_pairs[0, 0]
    second_idx = outage_pairs[0, 1]
    local_at = outage_ids[0] - me_state * half_len
    branch_iota = lax.broadcasted_iota(jnp.int32, (pair_count, half_len), 1)
    pick_branch = (branch_iota == local_at[:, None]).astype(jnp.bfloat16)
    flow_part = jnp.dot(
        pick_branch, base_real.astype(jnp.bfloat16), preferred_element_type=jnp.float32
    )
    pair_at = jnp.concatenate([first_idx, second_idx])
    pair_to = jnp.concatenate([second_idx, first_idx])
    outage_iota = lax.broadcasted_iota(jnp.int32, (2 * pair_count, pair_count), 1)
    pick_at = (outage_iota == pair_at[:, None]).astype(jnp.bfloat16)
    flow_pairs = jnp.dot(
        pick_at, flow_part.astype(jnp.bfloat16), preferred_element_type=jnp.float32
    ).reshape(2, pair_count)
    flow_other = lax.ppermute(
        flow_pairs, "state", [(j, (j + 1) % halves) for j in range(halves)]
    )
    coupled_rows = jnp.dot(pick_at, coupling[0], preferred_element_type=jnp.float32)
    coupled = jnp.sum(
        jnp.where(outage_iota == pair_to[:, None], coupled_rows, 0.0), axis=1
    ).reshape(2, pair_count)
    flows = flow_pairs + flow_other
    determinant = 1.0 - coupled[0] * coupled[1]
    w_first = (flows[0] + coupled[0] * flows[1]) / determinant
    w_second = (flows[1] + coupled[1] * flows[0]) / determinant
    packed = jnp.stack([w_first, w_second, first_idx.astype(jnp.float32), second_idx.astype(jnp.float32)])
    table = gather_doubling(packed.astype(jnp.bfloat16), ("blk",))

    state_local = jnp.stack(
        [base_real, base_reactive * base_reactive, voltage * rating], axis=1
    )
    other_half = lax.ppermute(
        state_local, "state", [(j, (j + 1) % halves) for j in range(halves)]
    )
    partner = [(j, (j + 1) % halves) for j in range(halves)]
    tiles_other = lax.ppermute(tile_values, "state", partner)
    ints_other = lax.ppermute(jnp.concatenate([monitored, tile_ids.reshape(-1)]), "state", partner)
    state_pos = jnp.concatenate([state_local, other_half])
    both_monitored = jnp.concatenate([monitored, ints_other[: monitored.shape[0]]])
    mon_at = (both_monitored - me_state * half_len) % (halves * half_len)
    all_vals = jnp.take(state_pos, mon_at, axis=0, mode="clip")
    mon_vals = all_vals[: monitored.shape[0]]
    other_vals = all_vals[monitored.shape[0]:]
    ids_other = ints_other[monitored.shape[0]:].reshape(tile_ids.shape)
    real_other = other_vals[:, 0].reshape(tiles_dev, tile_size)
    q_sq_other = other_vals[:, 1].reshape(tiles_dev, tile_size)
    inv_sq_other = 1.0 / (other_vals[:, 2] * other_vals[:, 2]).reshape(tiles_dev, tile_size)
    base_other = (real_other * real_other + q_sq_other) * inv_sq_other
    mon_real = mon_vals[:, 0].reshape(tiles_dev, tile_size)
    react_sq = mon_vals[:, 1].reshape(tiles_dev, tile_size)
    mon_limit = mon_vals[:, 2].reshape(tiles_dev, tile_size)
    inv_limit_sq = 1.0 / (mon_limit * mon_limit)
    base_sq = (mon_real * mon_real + react_sq) * inv_limit_sq

    neg = jnp.float32(-jnp.inf)
    block_iota = jnp.arange(blocks, dtype=jnp.int32)

    def slot_rows(ids):
        pick_block = (jnp.clip(ids, 0, blocks - 1).reshape(-1, 1) == block_iota[None, :]).astype(jnp.bfloat16)
        rows = jnp.dot(pick_block, table.reshape(blocks, -1), preferred_element_type=jnp.float32)
        return rows.astype(jnp.bfloat16).reshape(ids.shape + (4, pair_count))

    def slot_squares(values, rows, ids, real, q_sq, inv_sq):
        width = rows.shape[-1]
        rows_iota = lax.broadcasted_iota(jnp.int32, (1, 1, tile_size, width), 2)
        first_at = rows[:, :, 2].astype(jnp.int32)[:, :, None, :]
        second_at = rows[:, :, 3].astype(jnp.int32)[:, :, None, :]
        zero = jnp.zeros((), jnp.bfloat16)
        weights = jnp.where(rows_iota == first_at, rows[:, :, 0][:, :, None, :], zero) + jnp.where(
            rows_iota == second_at, rows[:, :, 1][:, :, None, :], zero
        )
        delta = jnp.einsum(
            "tkmi,tkip->tkmp", values, weights, preferred_element_type=jnp.float32
        )
        post = real[:, None, :, None] + delta
        squared = (post * post + q_sq[:, None, :, None]) * inv_sq[:, None, :, None]
        return jnp.where((ids >= 0)[:, :, None, None], squared, neg)

    def column_maxima(values, ids, real, q_sq, inv_sq, base):
        rows = lax.dynamic_slice_in_dim(slot_rows(ids), me_state * half_width, half_width, axis=3)
        col_max = jnp.max(slot_squares(values, rows, ids, real, q_sq, inv_sq), axis=2)
        matches = ids[:, :, None] == block_iota[None, None, :]
        worst = jnp.max(jnp.where(matches[:, :, :, None], col_max[:, :, None, :], neg), axis=(0, 1))
        absent = jnp.logical_not(jnp.any(matches, axis=1))
        absent_max = jnp.max(jnp.where(absent, jnp.max(base, axis=1)[:, None], neg), axis=0)
        return jnp.maximum(worst, absent_max[:, None])

    worst_local = jnp.maximum(
        column_maxima(tile_values, tile_ids, mon_real, react_sq, inv_limit_sq, base_sq),
        column_maxima(tiles_other, ids_other, real_other, q_sq_other, inv_sq_other, base_other),
    )
    worst_sq = scatter_max(worst_local, ("blk",))
    worst_own = jnp.sqrt(worst_sq)[None, :]

    any_absent = jnp.logical_not(
        jnp.all(jnp.any(tile_ids[:, :, None] == block_iota[None, None, :], axis=1), axis=1)
    )
    chosen = slot_rows(tile_ids)
    values_again, rows_again = lax.optimization_barrier((tile_values, chosen))
    peak_sq = jnp.max(slot_squares(values_again, rows_again, tile_ids, mon_real, react_sq, inv_limit_sq), axis=(1, 3))
    peak_sq = jnp.maximum(peak_sq, jnp.where(any_absent[:, None], base_sq, neg))
    peak_load = jnp.sqrt(peak_sq)
    return (peak_load.reshape(-1), worst_own)


def solution(mesh):
    return jax.shard_map(
        body,
        mesh=mesh,
        in_specs=(
            P(("cases", "blk", "state")),
            P(("cases", "blk", "state")),
            P(("cases", "blk", "state")),
            P(("cases", "blk", "state")),
            P(("cases", "blk", "state")),
            P(("cases", "blk", "state"), None),
            P(("cases", "blk", "state"), None, None, None),
            P(("cases", "blk"), None),
            P(("cases", "blk"), None, None),
            P(("cases", "blk"), None, None),
        ),
        out_specs=(P(("cases", "blk", "state")), P(("cases", "blk"), "state")),
        check_vma=False,
    )
```

```python
import jax
import jax.numpy as jnp
from jax import lax
from jax.sharding import PartitionSpec as P


def axes_size(axes):
    size = 1
    for axis in axes:
        size *= lax.axis_size(axis)
    return size


def gather_doubling(x, axes):
    n = axes_size(axes)
    me = lax.axis_index(axes)
    cur = x[None]
    bit = 1
    while bit < n:
        other = lax.ppermute(cur, axes, [(j, j ^ bit) for j in range(n)])
        low = (me & bit) == 0
        cur = jnp.where(low, jnp.concatenate([cur, other]), jnp.concatenate([other, cur]))
        bit *= 2
    return cur


def scatter_max(x, axes):
    n = axes_size(axes)
    me = lax.axis_index(axes)
    cur = x
    bit = n // 2
    while bit >= 1:
        pairs = cur.reshape((2, cur.shape[0] // 2) + cur.shape[1:])
        mine = (me // bit) % 2
        keep = lax.dynamic_index_in_dim(pairs, mine, 0, keepdims=False)
        send = lax.dynamic_index_in_dim(pairs, 1 - mine, 0, keepdims=False)
        got = lax.ppermute(send, axes, [(j, j ^ bit) for j in range(n)])
        cur = jnp.maximum(keep, got)
        bit //= 2
    return cur[0]


def body(
    base_real,
    base_reactive,
    voltage,
    rating,
    monitored,
    tile_ids,
    tile_values,
    outage_ids,
    coupling,
    outage_pairs,
):
    tiles_dev, slot_count, tile_size, _ = tile_values.shape
    pair_count = outage_pairs.shape[2]
    blocks = lax.axis_size("blk")
    halves = lax.axis_size("state")
    half_width = pair_count // halves
    half_len = base_real.shape[0]
    me_state = lax.axis_index("state")
    both = ("blk", "state")

    first_idx = outage_pairs[0, 0]
    second_idx = outage_pairs[0, 1]
    local_at = outage_ids[0] - me_state * half_len
    branch_iota = lax.broadcasted_iota(jnp.int32, (pair_count, half_len), 1)
    pick_branch = (branch_iota == local_at[:, None]).astype(jnp.bfloat16)
    flow_part = jnp.dot(
        pick_branch, base_real.astype(jnp.bfloat16), preferred_element_type=jnp.float32
    )
    pair_at = jnp.concatenate([first_idx, second_idx])
    pair_to = jnp.concatenate([second_idx, first_idx])
    outage_iota = lax.broadcasted_iota(jnp.int32, (2 * pair_count, pair_count), 1)
    pick_at = (outage_iota == pair_at[:, None]).astype(jnp.bfloat16)
    flow_pairs = jnp.dot(
        pick_at, flow_part.astype(jnp.bfloat16), preferred_element_type=jnp.float32
    ).reshape(2, pair_count)
    flow_other = lax.ppermute(
        flow_pairs, "state", [(j, (j + 1) % halves) for j in range(halves)]
    )
    coupled_rows = jnp.dot(pick_at, coupling[0], preferred_element_type=jnp.float32)
    coupled = jnp.sum(
        jnp.where(outage_iota == pair_to[:, None], coupled_rows, 0.0), axis=1
    ).reshape(2, pair_count)
    flows = flow_pairs + flow_other
    determinant = 1.0 - coupled[0] * coupled[1]
    w_first = (flows[0] + coupled[0] * flows[1]) / determinant
    w_second = (flows[1] + coupled[1] * flows[0]) / determinant
    packed = jnp.stack([w_first, w_second, first_idx.astype(jnp.float32), second_idx.astype(jnp.float32)])
    table = gather_doubling(packed.astype(jnp.bfloat16), ("blk",))

    state_local = jnp.stack([base_real, base_reactive * base_reactive, voltage * rating], axis=1)
    other_half = lax.ppermute(state_local, "state", [(j, (j + 1) % halves) for j in range(halves)])
    state_pos = jnp.concatenate([state_local, other_half])
    mon_at = (monitored - me_state * half_len) % (halves * half_len)
    mon_vals = jnp.take(state_pos, mon_at, axis=0, mode="clip")
    mon_real = mon_vals[:, 0].reshape(tiles_dev, tile_size)
    react_sq = mon_vals[:, 1].reshape(tiles_dev, tile_size)
    mon_limit = mon_vals[:, 2].reshape(tiles_dev, tile_size)
    inv_limit_sq = 1.0 / (mon_limit * mon_limit)
    base_sq = (mon_real * mon_real + react_sq) * inv_limit_sq

    valid = tile_ids >= 0
    block_of = jnp.clip(tile_ids, 0, blocks - 1)
    pick_block = (block_of.reshape(-1, 1) == jnp.arange(blocks, dtype=jnp.int32)[None, :]).astype(jnp.bfloat16)
    chosen = jnp.dot(pick_block, table.reshape(blocks, -1), preferred_element_type=jnp.float32)
    chosen = chosen.astype(jnp.bfloat16).reshape(tiles_dev, slot_count, 4, pair_count)
    neg = jnp.float32(-jnp.inf)

    def slot_squares(values, rows):
        rows_iota = lax.broadcasted_iota(jnp.int32, (1, 1, tile_size, pair_count), 2)
        first_at = rows[:, :, 2].astype(jnp.int32)[:, :, None, :]
        second_at = rows[:, :, 3].astype(jnp.int32)[:, :, None, :]
        zero = jnp.zeros((), jnp.bfloat16)
        weights = jnp.where(rows_iota == first_at, rows[:, :, 0][:, :, None, :], zero) + jnp.where(
            rows_iota == second_at, rows[:, :, 1][:, :, None, :], zero
        )
        delta = jnp.einsum(
            "tkmi,tkip->tkmp", values, weights, preferred_element_type=jnp.float32
        )
        post = mon_real[:, None, :, None] + delta
        squared = (post * post + react_sq[:, None, :, None]) * inv_limit_sq[:, None, :, None]
        return jnp.where(valid[:, :, None, None], squared, neg)

    squared = slot_squares(tile_values, chosen)

    block_iota = jnp.arange(blocks, dtype=jnp.int32)
    matches = tile_ids[:, :, None] == block_iota[None, None, :]
    absent = jnp.logical_not(jnp.any(matches, axis=1))
    any_absent = jnp.any(absent, axis=1)


    col_max = jnp.max(squared, axis=2)
    worst_local = jnp.max(
        jnp.where(matches[:, :, :, None], col_max[:, :, None, :], neg), axis=(0, 1)
    )
    base_max = jnp.max(base_sq, axis=1)
    absent_max = jnp.max(jnp.where(absent, base_max[:, None], neg), axis=0)
    worst_local = jnp.maximum(worst_local, absent_max[:, None])

    worst_sq = scatter_max(worst_local.reshape(blocks * halves, half_width), both)
    worst_own = jnp.sqrt(worst_sq)[None, :]
    values_again, rows_again = lax.optimization_barrier((tile_values, chosen))
    peak_sq = jnp.max(slot_squares(values_again, rows_again), axis=(1, 3))
    peak_sq = jnp.maximum(peak_sq, jnp.where(any_absent[:, None], base_sq, neg))
    peak_load = jnp.sqrt(peak_sq)
    return (peak_load.reshape(-1), worst_own)


def solution(mesh):
    return jax.shard_map(
        body,
        mesh=mesh,
        in_specs=(
            P(("cases", "blk", "state")),
            P(("cases", "blk", "state")),
            P(("cases", "blk", "state")),
            P(("cases", "blk", "state")),
            P(("cases", "blk", "state")),
            P(("cases", "blk", "state"), None),
            P(("cases", "blk", "state"), None, None, None),
            P(("cases", "blk"), None),
            P(("cases", "blk"), None, None),
            P(("cases", "blk"), None, None),
        ),
        out_specs=(P(("cases", "blk", "state")), P(("cases", "blk"), "state")),
        check_vma=False,
    )
```

```python
import jax
import jax.numpy as jnp
from jax import lax
from jax.sharding import PartitionSpec as P


def axes_size(axes):
    size = 1
    for axis in axes:
        size *= lax.axis_size(axis)
    return size


def gather_doubling(x, axes):
    n = axes_size(axes)
    me = lax.axis_index(axes)
    cur = x[None]
    bit = n // 2
    while bit >= 1:
        other = lax.ppermute(cur, axes, [(j, j ^ bit) for j in range(n)])
        low = (me & bit) == 0
        cur = jnp.where(low, jnp.stack([cur, other], axis=1), jnp.stack([other, cur], axis=1))
        cur = cur.reshape((-1,) + x.shape)
        bit //= 2
    return cur


def scatter_max(x, axes):
    n = axes_size(axes)
    me = lax.axis_index(axes)
    cur = x
    bit = n // 2
    while bit >= 1:
        pairs = cur.reshape((2, cur.shape[0] // 2) + cur.shape[1:])
        mine = (me // bit) % 2
        keep = lax.dynamic_index_in_dim(pairs, mine, 0, keepdims=False)
        send = lax.dynamic_index_in_dim(pairs, 1 - mine, 0, keepdims=False)
        got = lax.ppermute(send, axes, [(j, j ^ bit) for j in range(n)])
        cur = jnp.maximum(keep, got)
        bit //= 2
    return cur[0]


def body(
    base_real,
    base_reactive,
    voltage,
    rating,
    monitored,
    tile_ids,
    tile_values,
    outage_ids,
    coupling,
    outage_pairs,
):
    tiles_dev, slot_count, tile_size, _ = tile_values.shape
    pair_count = outage_pairs.shape[2]
    blocks = lax.axis_size("blk")
    halves = lax.axis_size("state")
    half_width = pair_count // halves
    half_len = base_real.shape[0]
    me_state = lax.axis_index("state")
    both = ("blk", "state")

    partner = [(j, (j + 1) % halves) for j in range(halves)]
    state_local = jnp.stack(
        [base_real, base_reactive * base_reactive, voltage * rating], axis=1
    )
    other_half = lax.ppermute(state_local, "state", partner)
    state_pos = jnp.concatenate([state_local, other_half])
    pos_len = halves * half_len

    first_idx = outage_pairs[0, 0]
    second_idx = outage_pairs[0, 1]
    outage_at = (outage_ids[0] - me_state * half_len) % pos_len
    branch_iota = lax.broadcasted_iota(jnp.int32, (pair_count, pos_len), 1)
    pick_branch = (branch_iota == outage_at[:, None]).astype(jnp.bfloat16)
    outage_flow = jnp.dot(
        pick_branch, state_pos[:, 0].astype(jnp.bfloat16), preferred_element_type=jnp.float32
    )
    pair_at = jnp.concatenate([first_idx, second_idx])
    pair_to = jnp.concatenate([second_idx, first_idx])
    outage_iota = lax.broadcasted_iota(jnp.int32, (2 * pair_count, pair_count), 1)
    pick_at = (outage_iota == pair_at[:, None]).astype(jnp.bfloat16)
    flows = jnp.dot(
        pick_at, outage_flow.astype(jnp.bfloat16), preferred_element_type=jnp.float32
    ).reshape(2, pair_count)
    coupled_rows = jnp.dot(pick_at, coupling[0], preferred_element_type=jnp.float32)
    coupled = jnp.sum(
        jnp.where(outage_iota == pair_to[:, None], coupled_rows, 0.0), axis=1
    ).reshape(2, pair_count)
    determinant = 1.0 - coupled[0] * coupled[1]
    w_first = (flows[0] + coupled[0] * flows[1]) / determinant
    w_second = (flows[1] + coupled[1] * flows[0]) / determinant
    packed = jnp.stack([w_first, w_second, first_idx.astype(jnp.float32), second_idx.astype(jnp.float32)])
    table = gather_doubling(packed.astype(jnp.bfloat16), ("blk",))

    mon_at = (monitored - me_state * half_len) % pos_len
    mon_vals = jnp.take(state_pos, mon_at, axis=0, mode="clip")
    mon_real = mon_vals[:, 0].reshape(tiles_dev, tile_size)
    react_sq = mon_vals[:, 1].reshape(tiles_dev, tile_size)
    mon_limit = mon_vals[:, 2].reshape(tiles_dev, tile_size)
    inv_limit_sq = 1.0 / (mon_limit * mon_limit)
    base_sq = (mon_real * mon_real + react_sq) * inv_limit_sq

    valid = tile_ids >= 0
    block_of = jnp.clip(tile_ids, 0, blocks - 1)
    pick_block = (block_of.reshape(-1, 1) == jnp.arange(blocks, dtype=jnp.int32)[None, :]).astype(jnp.bfloat16)
    chosen = jnp.dot(pick_block, table.reshape(blocks, -1), preferred_element_type=jnp.float32)
    chosen = chosen.astype(jnp.bfloat16).reshape(tiles_dev, slot_count, 4, pair_count)
    neg = jnp.float32(-jnp.inf)

    def slot_squares(values, rows):
        rows_iota = lax.broadcasted_iota(jnp.int32, (1, 1, tile_size, pair_count), 2)
        first_at = rows[:, :, 2].astype(jnp.int32)[:, :, None, :]
        second_at = rows[:, :, 3].astype(jnp.int32)[:, :, None, :]
        zero = jnp.zeros((), jnp.bfloat16)
        weights = jnp.where(rows_iota == first_at, rows[:, :, 0][:, :, None, :], zero) + jnp.where(
            rows_iota == second_at, rows[:, :, 1][:, :, None, :], zero
        )
        delta = jnp.einsum(
            "tkmi,tkip->tkmp", values, weights, preferred_element_type=jnp.float32
        )
        post = mon_real[:, None, :, None] + delta
        squared = (post * post + react_sq[:, None, :, None]) * inv_limit_sq[:, None, :, None]
        return jnp.where(valid[:, :, None, None], squared, neg)

    squared = slot_squares(tile_values, chosen)

    block_iota = jnp.arange(blocks, dtype=jnp.int32)
    matches = tile_ids[:, :, None] == block_iota[None, None, :]
    absent = jnp.logical_not(jnp.any(matches, axis=1))
    any_absent = jnp.any(absent, axis=1)


    col_max = jnp.max(squared, axis=2)
    worst_local = jnp.max(
        jnp.where(matches[:, :, :, None], col_max[:, :, None, :], neg), axis=(0, 1)
    )
    base_max = jnp.max(base_sq, axis=1)
    absent_max = jnp.max(jnp.where(absent, base_max[:, None], neg), axis=0)
    worst_local = jnp.maximum(worst_local, absent_max[:, None])

    worst_sq = scatter_max(worst_local.reshape(blocks * halves, half_width), both)
    worst_own = jnp.sqrt(worst_sq)[None, :]
    values_again, rows_again = lax.optimization_barrier((tile_values, chosen))
    peak_sq = jnp.max(slot_squares(values_again, rows_again), axis=(1, 3))
    peak_sq = jnp.maximum(peak_sq, jnp.where(any_absent[:, None], base_sq, neg))
    peak_load = jnp.sqrt(peak_sq)
    return (peak_load.reshape(-1), worst_own)


def solution(mesh):
    return jax.shard_map(
        body,
        mesh=mesh,
        in_specs=(
            P(("cases", "blk", "state")),
            P(("cases", "blk", "state")),
            P(("cases", "blk", "state")),
            P(("cases", "blk", "state")),
            P(("cases", "blk", "state")),
            P(("cases", "blk", "state"), None),
            P(("cases", "blk", "state"), None, None, None),
            P(("cases", "blk"), None),
            P(("cases", "blk"), None, None),
            P(("cases", "blk"), None, None),
        ),
        out_specs=(P(("cases", "blk", "state")), P(("cases", "blk"), "state")),
        check_vma=False,
    )
```

```python
import jax
import jax.numpy as jnp
from jax import lax
from jax.experimental import pallas as pl
from jax.experimental.pallas import tpu as pltpu
from jax.sharding import PartitionSpec as P


def axes_size(axes):
    size = 1
    for axis in axes:
        size *= lax.axis_size(axis)
    return size


def gather_doubling(x, axes):
    n = axes_size(axes)
    me = lax.axis_index(axes)
    cur = x[None]
    bit = n // 2
    while bit >= 1:
        other = lax.ppermute(cur, axes, [(j, j ^ bit) for j in range(n)])
        low = (me & bit) == 0
        cur = jnp.where(low, jnp.stack([cur, other], axis=1), jnp.stack([other, cur], axis=1))
        cur = cur.reshape((-1,) + x.shape)
        bit //= 2
    return cur


def scatter_max(x, axes):
    n = axes_size(axes)
    me = lax.axis_index(axes)
    cur = x
    bit = n // 2
    while bit >= 1:
        pairs = cur.reshape((2, cur.shape[0] // 2) + cur.shape[1:])
        mine = (me // bit) % 2
        keep = lax.dynamic_index_in_dim(pairs, mine, 0, keepdims=False)
        send = lax.dynamic_index_in_dim(pairs, 1 - mine, 0, keepdims=False)
        got = lax.ppermute(send, axes, [(j, j ^ bit) for j in range(n)])
        cur = jnp.maximum(keep, got)
        bit //= 2
    return cur[0]


def prep_kernel(me_ref, real_hbm, ids_hbm, pairs_hbm, coupling_hbm, flow_ref, coupled_ref,
                real_ref, ids_ref, pairs_ref, coupling_ref, sems):
    copies = [
        pltpu.make_async_copy(src, dst, sems.at[i])
        for i, (src, dst) in enumerate(
            ((real_hbm, real_ref), (ids_hbm, ids_ref), (pairs_hbm, pairs_ref), (coupling_hbm, coupling_ref))
        )
    ]
    for copy in copies:
        copy.start()
    for copy in copies:
        copy.wait()
    half_len = real_ref.shape[1]
    outages = ids_ref.shape[1]
    local_at = ids_ref[...] - me_ref[0] * half_len
    branch_iota = lax.broadcasted_iota(jnp.int32, (half_len, outages), 0)
    pick_branch = (branch_iota == local_at).astype(jnp.bfloat16)
    real = real_ref[...].astype(jnp.bfloat16)
    flow_part = jnp.dot(real, pick_branch, preferred_element_type=jnp.float32)
    pairs = pairs_ref[0]
    pair_at = jnp.concatenate([pairs[0:1], pairs[1:2]], axis=1)
    pair_to = jnp.concatenate([pairs[1:2], pairs[0:1]], axis=1)
    outage_iota = lax.broadcasted_iota(jnp.int32, (outages, pair_at.shape[1]), 0)
    pick_at = (outage_iota == pair_at).astype(jnp.bfloat16)
    flow_ref[...] = jnp.dot(
        flow_part.astype(jnp.bfloat16), pick_at, preferred_element_type=jnp.float32
    )
    columns = jnp.dot(coupling_ref[0], pick_at, preferred_element_type=jnp.float32)
    rows = (outage_iota == pair_to).astype(jnp.float32)
    coupled_ref[...] = jnp.sum(columns * rows, axis=0, keepdims=True)


def prep_call(me_state, base_real, outage_ids, outage_pairs, coupling):
    pair_count = outage_pairs.shape[2]
    real = base_real.reshape(1, -1)
    vmem = pl.BlockSpec(memory_space=pltpu.VMEM)
    anywhere = pl.BlockSpec(memory_space=pl.ANY)
    flow, coupled = pl.pallas_call(
        prep_kernel,
        out_shape=(
            jax.ShapeDtypeStruct((1, 2 * pair_count), jnp.float32),
            jax.ShapeDtypeStruct((1, 2 * pair_count), jnp.float32),
        ),
        in_specs=[pl.BlockSpec(memory_space=pltpu.SMEM), anywhere, anywhere, anywhere, anywhere],
        out_specs=(vmem, vmem),
        scratch_shapes=[
            pltpu.VMEM(real.shape, real.dtype),
            pltpu.VMEM(outage_ids.shape, outage_ids.dtype),
            pltpu.VMEM(outage_pairs.shape, outage_pairs.dtype),
            pltpu.VMEM(coupling.shape, coupling.dtype),
            pltpu.SemaphoreType.DMA((4,)),
        ],
    )(me_state.reshape(1), real, outage_ids, outage_pairs, coupling)
    return flow.reshape(2, pair_count), coupled.reshape(2, pair_count)[::-1]


def body(
    base_real,
    base_reactive,
    voltage,
    rating,
    monitored,
    tile_ids,
    tile_values,
    outage_ids,
    coupling,
    outage_pairs,
):
    tiles_dev, slot_count, tile_size, _ = tile_values.shape
    pair_count = outage_pairs.shape[2]
    blocks = lax.axis_size("blk")
    halves = lax.axis_size("state")
    half_width = pair_count // halves
    half_len = base_real.shape[0]
    me_state = lax.axis_index("state")
    both = ("blk", "state")

    first_idx = outage_pairs[0, 0]
    second_idx = outage_pairs[0, 1]
    flow_pairs, coupled = prep_call(me_state, base_real, outage_ids, outage_pairs, coupling)
    flow_other = lax.ppermute(
        flow_pairs, "state", [(j, (j + 1) % halves) for j in range(halves)]
    )
    flows = flow_pairs + flow_other
    determinant = 1.0 - coupled[0] * coupled[1]
    w_first = (flows[0] + coupled[0] * flows[1]) / determinant
    w_second = (flows[1] + coupled[1] * flows[0]) / determinant
    packed = jnp.stack([w_first, w_second, first_idx.astype(jnp.float32), second_idx.astype(jnp.float32)])
    table = gather_doubling(packed.astype(jnp.bfloat16), ("blk",))

    state_local = jnp.stack(
        [base_real, base_reactive * base_reactive, voltage * rating], axis=1
    )
    other_half = lax.ppermute(
        state_local, "state", [(j, (j + 1) % halves) for j in range(halves)]
    )
    state_pos = jnp.concatenate([state_local, other_half])
    mon_at = (monitored - me_state * half_len) % (halves * half_len)
    mon_vals = jnp.take(state_pos, mon_at, axis=0, mode="clip")
    mon_real = mon_vals[:, 0].reshape(tiles_dev, tile_size)
    react_sq = mon_vals[:, 1].reshape(tiles_dev, tile_size)
    mon_limit = mon_vals[:, 2].reshape(tiles_dev, tile_size)
    inv_limit_sq = 1.0 / (mon_limit * mon_limit)
    base_sq = (mon_real * mon_real + react_sq) * inv_limit_sq

    valid = tile_ids >= 0
    block_of = jnp.clip(tile_ids, 0, blocks - 1)
    pick_block = (block_of.reshape(-1, 1) == jnp.arange(blocks, dtype=jnp.int32)[None, :]).astype(jnp.bfloat16)
    chosen = jnp.dot(pick_block, table.reshape(blocks, -1), preferred_element_type=jnp.float32)
    chosen = chosen.astype(jnp.bfloat16).reshape(tiles_dev, slot_count, 4, pair_count)
    neg = jnp.float32(-jnp.inf)

    def slot_squares(values, rows):
        rows_iota = lax.broadcasted_iota(jnp.int32, (1, 1, tile_size, pair_count), 2)
        first_at = rows[:, :, 2].astype(jnp.int32)[:, :, None, :]
        second_at = rows[:, :, 3].astype(jnp.int32)[:, :, None, :]
        zero = jnp.zeros((), jnp.bfloat16)
        weights = jnp.where(rows_iota == first_at, rows[:, :, 0][:, :, None, :], zero) + jnp.where(
            rows_iota == second_at, rows[:, :, 1][:, :, None, :], zero
        )
        delta = jnp.einsum(
            "tkmi,tkip->tkmp", values, weights, preferred_element_type=jnp.float32
        )
        post = mon_real[:, None, :, None] + delta
        squared = (post * post + react_sq[:, None, :, None]) * inv_limit_sq[:, None, :, None]
        return jnp.where(valid[:, :, None, None], squared, neg)

    squared = slot_squares(tile_values, chosen)

    block_iota = jnp.arange(blocks, dtype=jnp.int32)
    matches = tile_ids[:, :, None] == block_iota[None, None, :]
    absent = jnp.logical_not(jnp.any(matches, axis=1))
    any_absent = jnp.any(absent, axis=1)


    col_max = jnp.max(squared, axis=2)
    worst_local = jnp.max(
        jnp.where(matches[:, :, :, None], col_max[:, :, None, :], neg), axis=(0, 1)
    )
    base_max = jnp.max(base_sq, axis=1)
    absent_max = jnp.max(jnp.where(absent, base_max[:, None], neg), axis=0)
    worst_local = jnp.maximum(worst_local, absent_max[:, None])

    worst_sq = scatter_max(worst_local.reshape(blocks * halves, half_width), both)
    worst_own = jnp.sqrt(worst_sq)[None, :]
    values_again, rows_again = lax.optimization_barrier((tile_values, chosen))
    peak_sq = jnp.max(slot_squares(values_again, rows_again), axis=(1, 3))
    peak_sq = jnp.maximum(peak_sq, jnp.where(any_absent[:, None], base_sq, neg))
    peak_load = jnp.sqrt(peak_sq)
    return (peak_load.reshape(-1), worst_own)


def solution(mesh):
    return jax.shard_map(
        body,
        mesh=mesh,
        in_specs=(
            P(("cases", "blk", "state")),
            P(("cases", "blk", "state")),
            P(("cases", "blk", "state")),
            P(("cases", "blk", "state")),
            P(("cases", "blk", "state")),
            P(("cases", "blk", "state"), None),
            P(("cases", "blk", "state"), None, None, None),
            P(("cases", "blk"), None),
            P(("cases", "blk"), None, None),
            P(("cases", "blk"), None, None),
        ),
        out_specs=(P(("cases", "blk", "state")), P(("cases", "blk"), "state")),
        check_vma=False,
    )
```

```python
import jax
import jax.numpy as jnp
from jax import lax
from jax.sharding import PartitionSpec as P


def axes_size(axes):
    size = 1
    for axis in axes:
        size *= lax.axis_size(axis)
    return size


def gather_doubling(x, axes):
    n = axes_size(axes)
    me = lax.axis_index(axes)
    cur = x[None]
    bit = n // 2
    while bit >= 1:
        other = lax.ppermute(cur, axes, [(j, j ^ bit) for j in range(n)])
        low = (me & bit) == 0
        cur = jnp.where(low, jnp.stack([cur, other], axis=1), jnp.stack([other, cur], axis=1))
        cur = cur.reshape((-1,) + x.shape)
        bit //= 2
    return cur


def scatter_max(x, axes):
    n = axes_size(axes)
    me = lax.axis_index(axes)
    cur = x
    bit = n // 2
    while bit >= 1:
        pairs = cur.reshape((2, cur.shape[0] // 2) + cur.shape[1:])
        mine = (me // bit) % 2
        keep = lax.dynamic_index_in_dim(pairs, mine, 0, keepdims=False)
        send = lax.dynamic_index_in_dim(pairs, 1 - mine, 0, keepdims=False)
        got = lax.ppermute(send, axes, [(j, j ^ bit) for j in range(n)])
        cur = jnp.maximum(keep, got)
        bit //= 2
    return cur[0]


def body(
    base_real,
    base_reactive,
    voltage,
    rating,
    monitored,
    tile_ids,
    tile_values,
    outage_ids,
    coupling,
    outage_pairs,
):
    tiles_dev, slot_count, tile_size, _ = tile_values.shape
    pair_count = outage_pairs.shape[2]
    blocks = lax.axis_size("blk")
    halves = lax.axis_size("state")
    half_width = pair_count // halves
    half_len = base_real.shape[0]
    me_state = lax.axis_index("state")
    both = ("blk", "state")

    first_idx = outage_pairs[0, 0]
    second_idx = outage_pairs[0, 1]
    partner = [(j, (j + 1) % halves) for j in range(halves)]
    real_other = lax.ppermute(base_real, "state", partner)
    pos_len = halves * half_len
    outage_at = (outage_ids[0] - me_state * half_len) % pos_len
    pair_at = jnp.concatenate([first_idx, second_idx])
    pair_to = jnp.concatenate([second_idx, first_idx])
    outage_iota = lax.broadcasted_iota(jnp.int32, (2 * pair_count, pair_count), 1)
    pick_at = (outage_iota == pair_at[:, None]).astype(jnp.bfloat16)
    coupled_rows = jnp.dot(pick_at, coupling[0], preferred_element_type=jnp.float32)
    coupled = jnp.sum(
        jnp.where(outage_iota == pair_to[:, None], coupled_rows, 0.0), axis=1
    ).reshape(2, pair_count)
    branch_iota = lax.broadcasted_iota(jnp.int32, (pair_count, pos_len), 1)
    pick_branch = (branch_iota == outage_at[:, None]).astype(jnp.bfloat16)
    real_pos = jnp.concatenate([base_real, real_other]).astype(jnp.bfloat16)
    outage_flow = jnp.dot(pick_branch, real_pos, preferred_element_type=jnp.float32)
    flows = jnp.dot(
        pick_at, outage_flow.astype(jnp.bfloat16), preferred_element_type=jnp.float32
    ).reshape(2, pair_count)
    determinant = 1.0 - coupled[0] * coupled[1]
    w_first = (flows[0] + coupled[0] * flows[1]) / determinant
    w_second = (flows[1] + coupled[1] * flows[0]) / determinant
    packed = jnp.stack([w_first, w_second, first_idx.astype(jnp.float32), second_idx.astype(jnp.float32)])
    table = gather_doubling(packed.astype(jnp.bfloat16), ("blk",))

    state_local = jnp.stack([base_real, base_reactive * base_reactive, voltage * rating], axis=1)
    other_half = lax.ppermute(state_local, "state", [(j, (j + 1) % halves) for j in range(halves)])
    state_pos = jnp.concatenate([state_local, other_half])
    mon_at = (monitored - me_state * half_len) % (halves * half_len)
    mon_vals = jnp.take(state_pos, mon_at, axis=0, mode="clip")
    mon_real = mon_vals[:, 0].reshape(tiles_dev, tile_size)
    react_sq = mon_vals[:, 1].reshape(tiles_dev, tile_size)
    mon_limit = mon_vals[:, 2].reshape(tiles_dev, tile_size)
    inv_limit_sq = 1.0 / (mon_limit * mon_limit)
    base_sq = (mon_real * mon_real + react_sq) * inv_limit_sq

    valid = tile_ids >= 0
    block_of = jnp.clip(tile_ids, 0, blocks - 1)
    pick_block = (block_of.reshape(-1, 1) == jnp.arange(blocks, dtype=jnp.int32)[None, :]).astype(jnp.bfloat16)
    chosen = jnp.dot(pick_block, table.reshape(blocks, -1), preferred_element_type=jnp.float32)
    chosen = chosen.astype(jnp.bfloat16).reshape(tiles_dev, slot_count, 4, pair_count)
    neg = jnp.float32(-jnp.inf)

    def slot_squares(values, rows):
        rows_iota = lax.broadcasted_iota(jnp.int32, (1, 1, tile_size, pair_count), 2)
        first_at = rows[:, :, 2].astype(jnp.int32)[:, :, None, :]
        second_at = rows[:, :, 3].astype(jnp.int32)[:, :, None, :]
        zero = jnp.zeros((), jnp.bfloat16)
        weights = jnp.where(rows_iota == first_at, rows[:, :, 0][:, :, None, :], zero) + jnp.where(
            rows_iota == second_at, rows[:, :, 1][:, :, None, :], zero
        )
        delta = jnp.einsum(
            "tkmi,tkip->tkmp", values, weights, preferred_element_type=jnp.float32
        )
        post = mon_real[:, None, :, None] + delta
        squared = (post * post + react_sq[:, None, :, None]) * inv_limit_sq[:, None, :, None]
        return jnp.where(valid[:, :, None, None], squared, neg)

    squared = slot_squares(tile_values, chosen)

    block_iota = jnp.arange(blocks, dtype=jnp.int32)
    matches = tile_ids[:, :, None] == block_iota[None, None, :]
    absent = jnp.logical_not(jnp.any(matches, axis=1))
    any_absent = jnp.any(absent, axis=1)


    col_max = jnp.max(squared, axis=2)
    worst_local = jnp.max(
        jnp.where(matches[:, :, :, None], col_max[:, :, None, :], neg), axis=(0, 1)
    )
    base_max = jnp.max(base_sq, axis=1)
    absent_max = jnp.max(jnp.where(absent, base_max[:, None], neg), axis=0)
    worst_local = jnp.maximum(worst_local, absent_max[:, None])

    worst_sq = scatter_max(worst_local.reshape(blocks * halves, half_width), both)
    worst_own = jnp.sqrt(worst_sq)[None, :]
    values_again, rows_again = lax.optimization_barrier((tile_values, chosen))
    peak_sq = jnp.max(slot_squares(values_again, rows_again), axis=(1, 3))
    peak_sq = jnp.maximum(peak_sq, jnp.where(any_absent[:, None], base_sq, neg))
    peak_load = jnp.sqrt(peak_sq)
    return (peak_load.reshape(-1), worst_own)


def solution(mesh):
    return jax.shard_map(
        body,
        mesh=mesh,
        in_specs=(
            P(("cases", "blk", "state")),
            P(("cases", "blk", "state")),
            P(("cases", "blk", "state")),
            P(("cases", "blk", "state")),
            P(("cases", "blk", "state")),
            P(("cases", "blk", "state"), None),
            P(("cases", "blk", "state"), None, None, None),
            P(("cases", "blk"), None),
            P(("cases", "blk"), None, None),
            P(("cases", "blk"), None, None),
        ),
        out_specs=(P(("cases", "blk", "state")), P(("cases", "blk"), "state")),
        check_vma=False,
    )
```

```python
import jax
import jax.numpy as jnp
from jax import lax
from jax.sharding import PartitionSpec as P


def axes_size(axes):
    size = 1
    for axis in axes:
        size *= lax.axis_size(axis)
    return size


def gather_doubling(x, axes):
    n = axes_size(axes)
    me = lax.axis_index(axes)
    cur = x[None]
    bit = n // 2
    while bit >= 1:
        other = lax.ppermute(cur, axes, [(j, j ^ bit) for j in range(n)])
        low = (me & bit) == 0
        cur = jnp.where(low, jnp.stack([cur, other], axis=1), jnp.stack([other, cur], axis=1))
        cur = cur.reshape((-1,) + x.shape)
        bit //= 2
    return cur


def scatter_max(x, axes):
    n = axes_size(axes)
    me = lax.axis_index(axes)
    cur = x
    bit = n // 2
    while bit >= 1:
        pairs = cur.reshape((2, cur.shape[0] // 2) + cur.shape[1:])
        mine = (me // bit) % 2
        keep = lax.dynamic_index_in_dim(pairs, mine, 0, keepdims=False)
        send = lax.dynamic_index_in_dim(pairs, 1 - mine, 0, keepdims=False)
        got = lax.ppermute(send, axes, [(j, j ^ bit) for j in range(n)])
        cur = jnp.maximum(keep, got)
        bit //= 2
    return cur[0]


def body(
    base_real,
    base_reactive,
    voltage,
    rating,
    monitored,
    tile_ids,
    tile_values,
    outage_ids,
    coupling,
    outage_pairs,
):
    tiles_dev, slot_count, tile_size, _ = tile_values.shape
    pair_count = outage_pairs.shape[2]
    blocks = lax.axis_size("blk")
    halves = lax.axis_size("state")
    half_width = pair_count // halves
    half_len = base_real.shape[0]
    me_state = lax.axis_index("state")
    both = ("blk", "state")

    first_idx = outage_pairs[0, 0]
    second_idx = outage_pairs[0, 1]
    local_at = outage_ids[0] - me_state * half_len
    branch_iota = lax.broadcasted_iota(jnp.int32, (pair_count, half_len), 1)
    pick_branch = (branch_iota == local_at[:, None]).astype(jnp.bfloat16)
    flow_part = jnp.dot(
        pick_branch, base_real.astype(jnp.bfloat16), preferred_element_type=jnp.float32
    )
    pair_at = jnp.concatenate([first_idx, second_idx])
    pair_to = jnp.concatenate([second_idx, first_idx])
    outage_iota = lax.broadcasted_iota(jnp.int32, (2 * pair_count, pair_count), 1)
    pick_at = (outage_iota == pair_at[:, None]).astype(jnp.bfloat16)
    flow_pairs = jnp.dot(
        pick_at, flow_part.astype(jnp.bfloat16), preferred_element_type=jnp.float32
    ).reshape(2, pair_count)
    flow_other = lax.ppermute(
        flow_pairs, "state", [(j, (j + 1) % halves) for j in range(halves)]
    )
    coupled_rows = jnp.dot(pick_at, coupling[0], preferred_element_type=jnp.float32)
    coupled = jnp.sum(
        jnp.where(outage_iota == pair_to[:, None], coupled_rows, 0.0), axis=1
    ).reshape(2, pair_count)
    flows = flow_pairs + flow_other
    determinant = 1.0 - coupled[0] * coupled[1]
    w_first = (flows[0] + coupled[0] * flows[1]) / determinant
    w_second = (flows[1] + coupled[1] * flows[0]) / determinant
    packed = jnp.stack([w_first, w_second, first_idx.astype(jnp.float32), second_idx.astype(jnp.float32)])
    table = gather_doubling(packed.astype(jnp.bfloat16), ("blk",))

    state_local = jnp.stack([base_real, base_reactive * base_reactive, voltage * rating], axis=1)
    other_half = lax.ppermute(state_local, "state", [(j, (j + 1) % halves) for j in range(halves)])
    state_pos = jnp.concatenate([state_local, other_half])
    mon_at = (monitored - me_state * half_len) % (halves * half_len)
    mon_vals = jnp.take(state_pos, mon_at, axis=0, mode="clip")
    mon_real = mon_vals[:, 0].reshape(tiles_dev, tile_size)
    react_sq = mon_vals[:, 1].reshape(tiles_dev, tile_size)
    mon_limit = mon_vals[:, 2].reshape(tiles_dev, tile_size)
    inv_limit_sq = 1.0 / (mon_limit * mon_limit)
    base_sq = (mon_real * mon_real + react_sq) * inv_limit_sq

    valid = tile_ids >= 0
    block_of = jnp.clip(tile_ids, 0, blocks - 1)
    pick_block = (block_of.reshape(-1, 1) == jnp.arange(blocks, dtype=jnp.int32)[None, :]).astype(jnp.bfloat16)
    chosen = jnp.dot(pick_block, table.reshape(blocks, -1), preferred_element_type=jnp.float32)
    chosen = chosen.astype(jnp.bfloat16).reshape(tiles_dev, slot_count, 4, pair_count)
    neg = jnp.float32(-jnp.inf)

    def slot_squares(values, rows):
        rows_iota = lax.broadcasted_iota(jnp.int32, (1, 1, tile_size, pair_count), 2)
        first_at = rows[:, :, 2].astype(jnp.int32)[:, :, None, :]
        second_at = rows[:, :, 3].astype(jnp.int32)[:, :, None, :]
        zero = jnp.zeros((), jnp.bfloat16)
        weights = jnp.where(rows_iota == first_at, rows[:, :, 0][:, :, None, :], zero) + jnp.where(
            rows_iota == second_at, rows[:, :, 1][:, :, None, :], zero
        )
        delta = jnp.einsum(
            "tkmi,tkip->tkmp", values, weights, preferred_element_type=jnp.float32
        )
        post = mon_real[:, None, :, None] + delta
        squared = (post * post + react_sq[:, None, :, None]) * inv_limit_sq[:, None, :, None]
        return jnp.where(valid[:, :, None, None], squared, neg)

    squared = slot_squares(tile_values, chosen)

    block_iota = jnp.arange(blocks, dtype=jnp.int32)
    matches = tile_ids[:, :, None] == block_iota[None, None, :]
    absent = jnp.logical_not(jnp.any(matches, axis=1))
    any_absent = jnp.any(absent, axis=1)
    base_max = jnp.max(base_sq, axis=1)
    absent_max = jnp.max(jnp.where(absent, base_max[:, None], neg), axis=0)


    col_max = jnp.max(squared, axis=2)
    worst_local = jnp.max(
        jnp.where(matches[:, :, :, None], col_max[:, :, None, :], neg), axis=(0, 1)
    )
    worst_local = jnp.maximum(worst_local, absent_max[:, None])

    worst_sq = scatter_max(worst_local.reshape(blocks * halves, half_width), both)
    worst_own = jnp.sqrt(worst_sq)[None, :]
    values_again, rows_again = lax.optimization_barrier((tile_values, chosen))
    peak_sq = jnp.max(slot_squares(values_again, rows_again), axis=(1, 3))
    peak_sq = jnp.maximum(peak_sq, jnp.where(any_absent[:, None], base_sq, neg))
    peak_load = jnp.sqrt(peak_sq)
    return (peak_load.reshape(-1), worst_own)


def solution(mesh):
    return jax.shard_map(
        body,
        mesh=mesh,
        in_specs=(
            P(("cases", "blk", "state")),
            P(("cases", "blk", "state")),
            P(("cases", "blk", "state")),
            P(("cases", "blk", "state")),
            P(("cases", "blk", "state")),
            P(("cases", "blk", "state"), None),
            P(("cases", "blk", "state"), None, None, None),
            P(("cases", "blk"), None),
            P(("cases", "blk"), None, None),
            P(("cases", "blk"), None, None),
        ),
        out_specs=(P(("cases", "blk", "state")), P(("cases", "blk"), "state")),
        check_vma=False,
    )
```

```python
import jax
import jax.numpy as jnp
from jax import lax
from jax.sharding import PartitionSpec as P


def axes_size(axes):
    size = 1
    for axis in axes:
        size *= lax.axis_size(axis)
    return size


def gather_doubling(x, axes):
    n = axes_size(axes)
    me = lax.axis_index(axes)
    cur = x[None]
    bit = n // 2
    while bit >= 1:
        other = lax.ppermute(cur, axes, [(j, j ^ bit) for j in range(n)])
        low = (me & bit) == 0
        cur = jnp.where(low, jnp.stack([cur, other], axis=1), jnp.stack([other, cur], axis=1))
        cur = cur.reshape((-1,) + x.shape)
        bit //= 2
    return cur


def scatter_max(x, axes):
    n = axes_size(axes)
    me = lax.axis_index(axes)
    cur = x
    bit = n // 2
    while bit >= 1:
        pairs = cur.reshape((2, cur.shape[0] // 2) + cur.shape[1:])
        mine = (me // bit) % 2
        keep = lax.dynamic_index_in_dim(pairs, mine, 0, keepdims=False)
        send = lax.dynamic_index_in_dim(pairs, 1 - mine, 0, keepdims=False)
        got = lax.ppermute(send, axes, [(j, j ^ bit) for j in range(n)])
        cur = jnp.maximum(keep, got)
        bit //= 2
    return cur[0]


def body(
    base_real,
    base_reactive,
    voltage,
    rating,
    monitored,
    tile_ids,
    tile_values,
    outage_ids,
    coupling,
    outage_pairs,
):
    tiles_dev, slot_count, tile_size, _ = tile_values.shape
    pair_count = outage_pairs.shape[2]
    blocks = lax.axis_size("blk")
    halves = lax.axis_size("state")
    half_width = pair_count // halves
    half_len = base_real.shape[0]
    me_state = lax.axis_index("state")
    both = ("blk", "state")

    first_idx = outage_pairs[0, 0]
    second_idx = outage_pairs[0, 1]
    local_at = outage_ids[0] - me_state * half_len
    branch_iota = lax.broadcasted_iota(jnp.int32, (pair_count, half_len), 1)
    pick_branch = (branch_iota == local_at[:, None]).astype(jnp.bfloat16)
    flow_part = jnp.dot(
        pick_branch, base_real.astype(jnp.bfloat16), preferred_element_type=jnp.float32
    )
    pair_at = jnp.concatenate([first_idx, second_idx])
    pair_to = jnp.concatenate([second_idx, first_idx])
    outage_iota = lax.broadcasted_iota(jnp.int32, (2 * pair_count, pair_count), 1)
    pick_at = (outage_iota == pair_at[:, None]).astype(jnp.bfloat16)
    flow_pairs = jnp.dot(
        pick_at, flow_part.astype(jnp.bfloat16), preferred_element_type=jnp.float32
    ).reshape(2, pair_count)
    flow_other = lax.ppermute(
        flow_pairs, "state", [(j, (j + 1) % halves) for j in range(halves)]
    )
    coupled_rows = jnp.dot(pick_at, coupling[0], preferred_element_type=jnp.float32)
    coupled = jnp.sum(
        jnp.where(outage_iota == pair_to[:, None], coupled_rows, 0.0), axis=1
    ).reshape(2, pair_count)
    flows = flow_pairs + flow_other
    determinant = 1.0 - coupled[0] * coupled[1]
    w_first = (flows[0] + coupled[0] * flows[1]) / determinant
    w_second = (flows[1] + coupled[1] * flows[0]) / determinant
    packed = jnp.stack([w_first, w_second, first_idx.astype(jnp.float32), second_idx.astype(jnp.float32)])
    table = gather_doubling(packed.astype(jnp.bfloat16), ("blk",))

    state_local = jnp.stack(
        [base_real, base_reactive * base_reactive, voltage * rating], axis=1
    )
    other_half = lax.ppermute(
        state_local, "state", [(j, (j + 1) % halves) for j in range(halves)]
    )
    state_pos = jnp.concatenate([state_local, other_half])
    mon_at = (monitored - me_state * half_len) % (halves * half_len)
    mon_vals = jnp.take(state_pos, mon_at, axis=0, mode="clip")
    mon_real = mon_vals[:, 0].reshape(tiles_dev, tile_size)
    react_sq = mon_vals[:, 1].reshape(tiles_dev, tile_size)
    mon_limit = mon_vals[:, 2].reshape(tiles_dev, tile_size)
    inv_limit_sq = 1.0 / (mon_limit * mon_limit)
    base_sq = (mon_real * mon_real + react_sq) * inv_limit_sq

    valid = tile_ids >= 0
    block_of = jnp.clip(tile_ids, 0, blocks - 1)
    pick_block = (block_of.reshape(-1, 1) == jnp.arange(blocks, dtype=jnp.int32)[None, :]).astype(jnp.bfloat16)
    chosen = jnp.dot(pick_block, table.reshape(blocks, -1), preferred_element_type=jnp.float32)
    chosen = chosen.astype(jnp.bfloat16).reshape(tiles_dev, slot_count, 4, pair_count)
    neg = jnp.float32(-jnp.inf)

    def slot_squares(values, rows):
        rows_iota = lax.broadcasted_iota(jnp.int32, (1, 1, tile_size, pair_count), 2)
        first_at = rows[:, :, 2].astype(jnp.int32)[:, :, None, :]
        second_at = rows[:, :, 3].astype(jnp.int32)[:, :, None, :]
        zero = jnp.zeros((), jnp.bfloat16)
        weights = jnp.where(rows_iota == first_at, rows[:, :, 0][:, :, None, :], zero) + jnp.where(
            rows_iota == second_at, rows[:, :, 1][:, :, None, :], zero
        )
        delta = jnp.einsum(
            "tkmi,tkip->tkmp", values, weights, preferred_element_type=jnp.float32
        )
        post = mon_real[:, None, :, None] + delta
        squared = (post * post + react_sq[:, None, :, None]) * inv_limit_sq[:, None, :, None]
        return jnp.where(valid[:, :, None, None], squared, neg)

    squared = slot_squares(tile_values, chosen)

    block_iota = jnp.arange(blocks, dtype=jnp.int32)
    matches = tile_ids[:, :, None] == block_iota[None, None, :]
    absent = jnp.logical_not(jnp.any(matches, axis=1))
    any_absent = jnp.any(absent, axis=1)


    col_max = jnp.max(squared, axis=2)
    worst_local = jnp.max(
        jnp.where(matches[:, :, :, None], col_max[:, :, None, :], neg), axis=(0, 1)
    )
    base_max = jnp.max(base_sq, axis=1)
    absent_max = jnp.max(jnp.where(absent, base_max[:, None], neg), axis=0)
    worst_local = jnp.maximum(worst_local, absent_max[:, None])

    worst_own = scatter_max(jnp.sqrt(worst_local).reshape(blocks * halves, half_width), both)[None, :]
    values_again, rows_again = lax.optimization_barrier((tile_values, chosen))
    peak_sq = jnp.max(slot_squares(values_again, rows_again), axis=(1, 3))
    peak_sq = jnp.maximum(peak_sq, jnp.where(any_absent[:, None], base_sq, neg))
    peak_load = jnp.sqrt(peak_sq)
    return (peak_load.reshape(-1), worst_own)


def solution(mesh):
    return jax.shard_map(
        body,
        mesh=mesh,
        in_specs=(
            P(("cases", "blk", "state")),
            P(("cases", "blk", "state")),
            P(("cases", "blk", "state")),
            P(("cases", "blk", "state")),
            P(("cases", "blk", "state")),
            P(("cases", "blk", "state"), None),
            P(("cases", "blk", "state"), None, None, None),
            P(("cases", "blk"), None),
            P(("cases", "blk"), None, None),
            P(("cases", "blk"), None, None),
        ),
        out_specs=(P(("cases", "blk", "state")), P(("cases", "blk"), "state")),
        check_vma=False,
    )
```

```python
import jax
import jax.numpy as jnp
from jax import lax
from jax.sharding import PartitionSpec as P


def axes_size(axes):
    size = 1
    for axis in axes:
        size *= lax.axis_size(axis)
    return size


def gather_doubling(x, axes):
    n = axes_size(axes)
    me = lax.axis_index(axes)
    cur = x[None]
    bit = n // 2
    while bit >= 2:
        other = lax.ppermute(cur, axes, [(j, j ^ bit) for j in range(n)])
        low = (me & bit) == 0
        cur = jnp.where(low, jnp.stack([cur, other], axis=1), jnp.stack([other, cur], axis=1))
        cur = cur.reshape((-1,) + x.shape)
        bit //= 2
    other = lax.ppermute(cur, axes, [(j, j ^ 1) for j in range(n)])
    return cur, other


def scatter_max(x, axes):
    n = axes_size(axes)
    me = lax.axis_index(axes)
    cur = x
    bit = n // 2
    while bit >= 1:
        pairs = cur.reshape((2, cur.shape[0] // 2) + cur.shape[1:])
        mine = (me // bit) % 2
        keep = lax.dynamic_index_in_dim(pairs, mine, 0, keepdims=False)
        send = lax.dynamic_index_in_dim(pairs, 1 - mine, 0, keepdims=False)
        got = lax.ppermute(send, axes, [(j, j ^ bit) for j in range(n)])
        cur = jnp.maximum(keep, got)
        bit //= 2
    return cur[0]


def body(
    base_real,
    base_reactive,
    voltage,
    rating,
    monitored,
    tile_ids,
    tile_values,
    outage_ids,
    coupling,
    outage_pairs,
):
    tiles_dev, slot_count, tile_size, _ = tile_values.shape
    pair_count = outage_pairs.shape[2]
    blocks = lax.axis_size("blk")
    halves = lax.axis_size("state")
    half_width = pair_count // halves
    half_len = base_real.shape[0]
    me_state = lax.axis_index("state")
    both = ("blk", "state")

    first_idx = outage_pairs[0, 0]
    second_idx = outage_pairs[0, 1]
    local_at = outage_ids[0] - me_state * half_len
    branch_iota = lax.broadcasted_iota(jnp.int32, (pair_count, half_len), 1)
    pick_branch = (branch_iota == local_at[:, None]).astype(jnp.bfloat16)
    flow_part = jnp.dot(
        pick_branch, base_real.astype(jnp.bfloat16), preferred_element_type=jnp.float32
    )
    pair_at = jnp.concatenate([first_idx, second_idx])
    pair_to = jnp.concatenate([second_idx, first_idx])
    outage_iota = lax.broadcasted_iota(jnp.int32, (2 * pair_count, pair_count), 1)
    pick_at = (outage_iota == pair_at[:, None]).astype(jnp.bfloat16)
    flow_pairs = jnp.dot(
        pick_at, flow_part.astype(jnp.bfloat16), preferred_element_type=jnp.float32
    ).reshape(2, pair_count)
    flow_other = lax.ppermute(
        flow_pairs, "state", [(j, (j + 1) % halves) for j in range(halves)]
    )
    coupled_rows = jnp.dot(pick_at, coupling[0], preferred_element_type=jnp.float32)
    coupled = jnp.sum(
        jnp.where(outage_iota == pair_to[:, None], coupled_rows, 0.0), axis=1
    ).reshape(2, pair_count)
    flows = flow_pairs + flow_other
    determinant = 1.0 - coupled[0] * coupled[1]
    w_first = (flows[0] + coupled[0] * flows[1]) / determinant
    w_second = (flows[1] + coupled[1] * flows[0]) / determinant
    packed = jnp.stack([w_first, w_second, first_idx.astype(jnp.float32), second_idx.astype(jnp.float32)])
    own_rows, other_rows = gather_doubling(packed.astype(jnp.bfloat16), ("blk",))
    me_low = lax.axis_index("blk") % 2

    state_local = jnp.stack([base_real, base_reactive * base_reactive, voltage * rating], axis=1)
    other_half = lax.ppermute(state_local, "state", [(j, (j + 1) % halves) for j in range(halves)])
    state_pos = jnp.concatenate([state_local, other_half])
    mon_at = (monitored - me_state * half_len) % (halves * half_len)
    mon_vals = jnp.take(state_pos, mon_at, axis=0, mode="clip")
    mon_real = mon_vals[:, 0].reshape(tiles_dev, tile_size)
    react_sq = mon_vals[:, 1].reshape(tiles_dev, tile_size)
    mon_limit = mon_vals[:, 2].reshape(tiles_dev, tile_size)
    inv_limit_sq = 1.0 / (mon_limit * mon_limit)
    base_sq = (mon_real * mon_real + react_sq) * inv_limit_sq

    valid = tile_ids >= 0
    block_of = jnp.clip(tile_ids, 0, blocks - 1)
    row_iota = jnp.arange(blocks // 2, dtype=jnp.int32)[None, :]
    at_row = block_of.reshape(-1, 1) // 2 == row_iota
    mine_low = (block_of.reshape(-1, 1) % 2) == me_low
    pick_own = (at_row & mine_low).astype(jnp.bfloat16)
    pick_other = (at_row & jnp.logical_not(mine_low)).astype(jnp.bfloat16)
    chosen = jnp.dot(pick_own, own_rows.reshape(blocks // 2, -1), preferred_element_type=jnp.float32) + jnp.dot(
        pick_other, other_rows.reshape(blocks // 2, -1), preferred_element_type=jnp.float32
    )
    chosen = chosen.astype(jnp.bfloat16).reshape(tiles_dev, slot_count, 4, pair_count)
    neg = jnp.float32(-jnp.inf)

    def slot_squares(values, rows):
        rows_iota = lax.broadcasted_iota(jnp.int32, (1, 1, tile_size, pair_count), 2)
        first_at = rows[:, :, 2].astype(jnp.int32)[:, :, None, :]
        second_at = rows[:, :, 3].astype(jnp.int32)[:, :, None, :]
        zero = jnp.zeros((), jnp.bfloat16)
        weights = jnp.where(rows_iota == first_at, rows[:, :, 0][:, :, None, :], zero) + jnp.where(
            rows_iota == second_at, rows[:, :, 1][:, :, None, :], zero
        )
        delta = jnp.einsum(
            "tkmi,tkip->tkmp", values, weights, preferred_element_type=jnp.float32
        )
        post = mon_real[:, None, :, None] + delta
        squared = (post * post + react_sq[:, None, :, None]) * inv_limit_sq[:, None, :, None]
        return jnp.where(valid[:, :, None, None], squared, neg)

    squared = slot_squares(tile_values, chosen)

    block_iota = jnp.arange(blocks, dtype=jnp.int32)
    matches = tile_ids[:, :, None] == block_iota[None, None, :]
    absent = jnp.logical_not(jnp.any(matches, axis=1))
    any_absent = jnp.any(absent, axis=1)


    col_max = jnp.max(squared, axis=2)
    worst_local = jnp.max(
        jnp.where(matches[:, :, :, None], col_max[:, :, None, :], neg), axis=(0, 1)
    )
    base_max = jnp.max(base_sq, axis=1)
    absent_max = jnp.max(jnp.where(absent, base_max[:, None], neg), axis=0)
    worst_local = jnp.maximum(worst_local, absent_max[:, None])

    worst_sq = scatter_max(worst_local.reshape(blocks * halves, half_width), both)
    worst_own = jnp.sqrt(worst_sq)[None, :]
    values_again, rows_again = lax.optimization_barrier((tile_values, chosen))
    peak_sq = jnp.max(slot_squares(values_again, rows_again), axis=(1, 3))
    peak_sq = jnp.maximum(peak_sq, jnp.where(any_absent[:, None], base_sq, neg))
    peak_load = jnp.sqrt(peak_sq)
    return (peak_load.reshape(-1), worst_own)


def solution(mesh):
    return jax.shard_map(
        body,
        mesh=mesh,
        in_specs=(
            P(("cases", "blk", "state")),
            P(("cases", "blk", "state")),
            P(("cases", "blk", "state")),
            P(("cases", "blk", "state")),
            P(("cases", "blk", "state")),
            P(("cases", "blk", "state"), None),
            P(("cases", "blk", "state"), None, None, None),
            P(("cases", "blk"), None),
            P(("cases", "blk"), None, None),
            P(("cases", "blk"), None, None),
        ),
        out_specs=(P(("cases", "blk", "state")), P(("cases", "blk"), "state")),
        check_vma=False,
    )
```
